32 devices in a mesh: groups: 2 (over y), seq: 8 (over z, x), hid: 2 (over core).
Axes of the slice: x: 2, y: 2, z: 4, core: 2. Of those that a mesh axis runs over, the one named last changes fastest.
Arguments:
- tokens: bfloat16 [2048, 2048], P(('groups', 'seq'), 'hid'), parts along dimension 0, may hold values from -6 to 6
- cotangent: bfloat16 [2048, 2048], P(('groups', 'seq'), 'hid'), parts along dimension 0, may hold values from -6 to 6
- blocks: bfloat16 [8, 128, 128], P('seq'), may hold values from -0.5 to 0.5
- coef_self: float32 [3, 1024], P(None, 'seq'), may hold values from 0.7 to 1
- coef_cross: float32 [3, 1024], P(None, 'seq'), may hold values from -0.5 to 0.5
- norm_gain: float32 [2048], P('hid'), may hold values from 0.5 to 1.5
- w_gate: bfloat16 [16, 128, 512], P('hid'), may hold values from -0.5 to 0.5
- w_up: bfloat16 [16, 128, 512], P('hid'), may hold values from -0.5 to 0.5
- w_down: bfloat16 [16, 512, 128], P('hid'), may hold values from -0.25 to 0.25
Outputs:
- grad_x: bfloat16 [2048, 2048], P(('groups', 'seq'), 'hid'), parts along dimension 0
- grad_self: float32 [3, 2048], P(None, ('groups', 'seq')), parts along dimension 1
- grad_cross: float32 [3, 2048], P(None, ('groups', 'seq')), parts along dimension 1
- grad_blocks: float32 [16, 128, 128], P(('groups', 'seq')), parts along dimension 0
The draws below stay inside these ranges and needn't reach their ends.
There are 2 independent parts, one for each index of `groups`. The reference program is written for one: setup_inputs(seed, part) draws one part's arguments, and reference() takes and returns one part's arrays. A program takes and returns all parts, laid end to end along the dimension named above; an argument that names none is the same for every part. Nothing has to cross between parts.
All inputs are finite; a program needn't handle non-finite values.
Results may differ from the reference program's by a relative error of at most 0.0097.
Values may be sent and summed in bfloat16 or wider, within the bound.
No kernel may reach another device: no remote copies, remote signals or barrier semaphores. Data moves between devices by JAX's collectives and lax.ppermute only.
A program may use at most 64 MiB of HBM per device.

```python
import jax
import jax.numpy as jnp
from jax import lax

D = 2048
CB = 128
E = 512
BLOCK = 128
TOK_DEV = 128
TOKENS = 1024
SECTIONS = 3
NB = 8
G = 16


def shard_levels(own_key, extent, shards, smallest, high):
    def one(axis_at, blocks):
        draws = jax.random.uniform(jax.random.fold_in(jax.random.fold_in(own_key, 6), axis_at), (blocks,), jnp.float32, smallest / len(shards), high / len(shards))
        return jnp.repeat(jnp.exp(draws), extent[axis_at] // blocks).reshape((-1,) + (1,) * (len(extent) - axis_at - 1))

    level = one(*shards[0])
    for cut in shards[1:]:
        level = level * one(*cut)
    return level


def normal_values(key, shape, scale, limit, split=(), kind=jnp.bfloat16):
    values = scale * jax.random.normal(key, shape, jnp.float32)
    if split:
        values = values * shard_levels(key, shape, split, -0.22, 0.18)
    return jnp.clip(values, -limit, limit).astype(kind)


def setup_inputs(seed: int = 0, part: int = 0) -> dict:
    streams_of = jax.random.split(jax.random.key(seed), 10)
    part_splits = jax.random.split(jax.random.fold_in(streams_of[9], part), 10)
    tokens = normal_values(part_splits[0], (TOKENS, D), 1.0, 6.0, ((0, 8), (1, 2)))
    cotangent = normal_values(part_splits[1], (TOKENS, D), 1.0, 6.0, ((0, 8), (1, 2)))
    blocks = normal_values(streams_of[2], (NB, BLOCK, BLOCK), BLOCK ** -0.5, 0.5, ((0, 8),))
    coef_self = jnp.clip(0.7 + 0.3 * jax.random.uniform(streams_of[3], (SECTIONS, TOKENS), jnp.float32) ** shard_levels(streams_of[3], (SECTIONS, TOKENS), ((1, 8),), -0.2, 0.2), 0.7, 1.0)
    coef_cross = jnp.clip(jax.random.uniform(streams_of[4], (SECTIONS, TOKENS), jnp.float32, -0.5, 0.5) * shard_levels(streams_of[4], (SECTIONS, TOKENS), ((1, 8),), -0.4, 0.0), -0.5, 0.5)
    norm_gain = jnp.clip(1.0 + 0.1 * jax.random.normal(streams_of[5], (D,), jnp.float32), 0.5, 1.5)
    w_gate = normal_values(streams_of[6], (G, CB, E), CB ** -0.5, 0.5, ((0, 2),))
    w_up = normal_values(streams_of[7], (G, CB, E), CB ** -0.5, 0.5, ((0, 2),))
    w_down = normal_values(streams_of[8], (G, E, CB), E ** -0.5, 0.25, ((0, 2),))
    return dict(tokens=tokens, cotangent=cotangent, blocks=blocks, coef_self=coef_self, coef_cross=coef_cross, norm_gain=norm_gain, w_gate=w_gate, w_up=w_up, w_down=w_down)


def flip_pairs(values, span):
    length, width = values.shape
    shaped = values.reshape(length // (2 * span), 2, span, width)
    return shaped[:, ::-1].reshape(length, width)

def reference(tokens, cotangent, blocks, coef_self, coef_cross, norm_gain, w_gate, w_up, w_down):
    length, width = tokens.shape
    nblk = length // BLOCK
    tok_f = tokens.astype(jnp.float32)
    tok_blocks = tok_f.reshape(nblk, BLOCK, width)
    blk_f = blocks.astype(jnp.float32)
    local = jnp.einsum('kij,kjd->kid', blk_f, tok_blocks).astype(jnp.bfloat16).reshape(length, width)
    states = []
    mates = []
    current = local
    for section in range(SECTIONS):
        span = TOK_DEV * 2 ** section
        mate = flip_pairs(current, span)
        states.append(current)
        mates.append(mate)
        current = (coef_self[section][:, None] * current.astype(jnp.float32) + coef_cross[section][:, None] * mate.astype(jnp.float32)).astype(jnp.bfloat16)
    mixed = current.astype(jnp.float32)
    resid = tok_f + tok_f * mixed
    inv = jax.lax.rsqrt(lax.optimization_barrier(jnp.sum(resid * resid, axis=-1)) / D + 1e-06)
    normed = (resid * inv[:, None] * norm_gain).astype(jnp.bfloat16)
    normed_b = normed.astype(jnp.float32).reshape(length, G, CB)
    gate_pre = jnp.einsum('tgc,gce->tge', normed_b, w_gate.astype(jnp.float32))
    up_val = jnp.einsum('tgc,gce->tge', normed_b, w_up.astype(jnp.float32))
    cot_f = cotangent.astype(jnp.float32)
    d_hidden = jnp.einsum('tgc,gec->tge', cot_f.reshape(length, G, CB), w_down.astype(jnp.float32))
    sig = jax.nn.sigmoid(gate_pre)
    d_up = (d_hidden * gate_pre * sig).astype(jnp.bfloat16).astype(jnp.float32)
    d_gate = (d_hidden * up_val * sig * (1.0 + gate_pre * (1.0 - sig))).astype(jnp.bfloat16).astype(jnp.float32)
    d_normed = jnp.einsum('tge,gce->tgc', d_gate, w_gate.astype(jnp.float32)) + jnp.einsum('tge,gce->tgc', d_up, w_up.astype(jnp.float32))
    scaled = norm_gain * d_normed.reshape(length, width)
    inner = lax.optimization_barrier(jnp.sum(resid * scaled, axis=-1))
    d_resid = cot_f + inv[:, None] * scaled - resid * (inv ** 3 * inner / D)[:, None]
    d_mixed = (d_resid * tok_f).astype(jnp.bfloat16)
    back = d_mixed
    grads_self = [None] * SECTIONS
    grads_cross = [None] * SECTIONS
    for section in range(SECTIONS - 1, -1, -1):
        span = TOK_DEV * 2 ** section
        back_f = back.astype(jnp.float32)
        grads_self[section] = lax.optimization_barrier(jnp.sum(back_f * states[section].astype(jnp.float32), axis=-1))
        grads_cross[section] = lax.optimization_barrier(jnp.sum(back_f * mates[section].astype(jnp.float32), axis=-1))
        sent = (coef_cross[section][:, None] * back_f).astype(jnp.bfloat16)
        back = (coef_self[section][:, None] * back_f + flip_pairs(sent, span).astype(jnp.float32)).astype(jnp.bfloat16)
    back_blocks = back.astype(jnp.float32).reshape(nblk, BLOCK, width)
    grad_blocks = jnp.einsum('kid,kjd->kij', back_blocks, tok_blocks)
    from_blocks = jnp.einsum('kij,kid->kjd', blk_f, back_blocks).reshape(length, width)
    grad_x = (d_resid * (1.0 + mixed) + from_blocks).astype(jnp.bfloat16)
    return (grad_x, jnp.stack(grads_self), jnp.stack(grads_cross), grad_blocks)
```

```python
import jax
import jax.numpy as jnp
from jax import lax
from jax.sharding import PartitionSpec as P

D = 2048


def from_partner(value, axis, distance):
    mask = 2**distance
    pairs = [(source, source ^ mask) for source in range(lax.axis_size(axis))]
    return lax.ppermute(value, axis, pairs)


def hid_sum(value):
    size = lax.axis_size("hid")
    total = value
    for shift in range(1, size):
        pairs = [(source, (source + shift) % size) for source in range(size)]
        total = total + lax.ppermute(value, "hid", pairs)
    return total


def body(tokens, cotangent, blocks, coef_self, coef_cross, norm_gain, w_gate, w_up, w_down):
    tok, width = tokens.shape
    sections = lax.axis_size("seq").bit_length() - 1
    nblk = blocks.shape[0]
    blen = blocks.shape[1]
    groups_here = w_gate.shape[0]
    cblock = w_gate.shape[1]
    tok_blocks = tokens.reshape(nblk, blen, width)
    local = jnp.einsum("kij,kjd->kid", blocks, tok_blocks, preferred_element_type=jnp.float32)
    local = local.astype(jnp.bfloat16).reshape(tok, width)
    states = []
    mates = []
    current = local
    for section in range(sections):
        mate = from_partner(current, "seq", section)
        states.append(current)
        mates.append(mate)
        current = (
            coef_self[section][:, None] * current.astype(jnp.float32)
            + coef_cross[section][:, None] * mate.astype(jnp.float32)
        ).astype(jnp.bfloat16)
    tok_f = tokens.astype(jnp.float32)
    mixed_f = current.astype(jnp.float32)
    resid = tok_f + tok_f * mixed_f
    square = hid_sum(jnp.sum(resid * resid, axis=-1))
    inv = lax.rsqrt(square / D + 1e-06)
    normed = (
        (resid * inv[:, None] * norm_gain).astype(jnp.bfloat16).reshape(tok, groups_here, cblock)
    )
    gate_pre = jnp.einsum("tgc,gce->tge", normed, w_gate, preferred_element_type=jnp.float32)
    up_val = jnp.einsum("tgc,gce->tge", normed, w_up, preferred_element_type=jnp.float32)
    d_hidden = jnp.einsum(
        "tgc,gec->tge",
        cotangent.reshape(tok, groups_here, cblock),
        w_down,
        preferred_element_type=jnp.float32,
    )
    sig = jax.nn.sigmoid(gate_pre)
    d_up = (d_hidden * gate_pre * sig).astype(jnp.bfloat16)
    d_gate = (d_hidden * up_val * sig * (1.0 + gate_pre * (1.0 - sig))).astype(jnp.bfloat16)
    d_normed = jnp.einsum("tge,gce->tgc", d_gate, w_gate, preferred_element_type=jnp.float32)
    d_normed = d_normed + jnp.einsum("tge,gce->tgc", d_up, w_up, preferred_element_type=jnp.float32)
    scaled = norm_gain * d_normed.reshape(tok, width)
    inner = hid_sum(jnp.sum(resid * scaled, axis=-1))
    d_resid = (
        cotangent.astype(jnp.float32)
        + inv[:, None] * scaled
        - resid * (inv**3 * inner / D)[:, None]
    )
    d_mixed = (d_resid * tok_f).astype(jnp.bfloat16)
    grads_self = [None] * sections
    grads_cross = [None] * sections
    back = d_mixed
    for section in range(sections - 1, -1, -1):
        back_f = back.astype(jnp.float32)
        grads_self[section] = jnp.sum(back_f * states[section].astype(jnp.float32), axis=-1)
        grads_cross[section] = jnp.sum(back_f * mates[section].astype(jnp.float32), axis=-1)
        sent = (coef_cross[section][:, None] * back_f).astype(jnp.bfloat16)
        received = from_partner(sent, "seq", section)
        back = (coef_self[section][:, None] * back_f + received.astype(jnp.float32)).astype(
            jnp.bfloat16
        )
    part_self = jnp.stack(grads_self)
    part_cross = jnp.stack(grads_cross)
    back_blocks = back.reshape(nblk, blen, width)
    part_blocks = jnp.einsum(
        "kid,kjd->kij", back_blocks, tok_blocks, preferred_element_type=jnp.float32
    )
    from_blocks = jnp.einsum(
        "kij,kid->kjd", blocks, back_blocks, preferred_element_type=jnp.float32
    ).reshape(tok, width)
    grad_self, grad_cross, grad_blocks = jax.tree.map(hid_sum, (part_self, part_cross, part_blocks))
    grad_x = (d_resid * (1.0 + mixed_f) + from_blocks).astype(jnp.bfloat16)
    return (grad_x, grad_self, grad_cross, grad_blocks)


def solution(mesh):
    return jax.shard_map(
        body,
        mesh=mesh,
        in_specs=(
            P(("groups", "seq"), "hid"),
            P(("groups", "seq"), "hid"),
            P("seq", None, None),
            P(None, "seq"),
            P(None, "seq"),
            P("hid"),
            P("hid", None, None),
            P("hid", None, None),
            P("hid", None, None),
        ),
        out_specs=(
            P(("groups", "seq"), "hid"),
            P(None, ("groups", "seq")),
            P(None, ("groups", "seq")),
            P(("groups", "seq"), None, None),
        ),
        check_vma=False,
    )
```

```python
import jax
import jax.numpy as jnp
from jax import lax
from jax.sharding import PartitionSpec as P

D = 2048
CHUNKS = 2


def from_partner(value, axis, distance):
    mask = 2**distance
    pairs = [(source, source ^ mask) for source in range(lax.axis_size(axis))]
    return lax.ppermute(value, axis, pairs)


def hid_sum(value):
    size = lax.axis_size("hid")
    total = value
    for shift in range(1, size):
        pairs = [(source, (source + shift) % size) for source in range(size)]
        total = total + lax.ppermute(value, "hid", pairs)
    return total


def chain(local, tokens, cotangent, coef_self, coef_cross, norm_gain, w_gate, w_up, w_down):
    tok, width = tokens.shape
    sections = coef_self.shape[0]
    groups_here = w_gate.shape[0]
    cblock = w_gate.shape[1]
    states = []
    mates = []
    current = local
    for section in range(sections):
        mate = from_partner(current, "seq", section)
        states.append(current)
        mates.append(mate)
        current = (
            coef_self[section][:, None] * current.astype(jnp.float32)
            + coef_cross[section][:, None] * mate.astype(jnp.float32)
        ).astype(jnp.bfloat16)
    tok_f = tokens.astype(jnp.float32)
    mixed_f = current.astype(jnp.float32)
    resid = tok_f + tok_f * mixed_f
    square = hid_sum(jnp.sum(resid * resid, axis=-1))
    inv = lax.rsqrt(square / D + 1e-06)
    normed = (
        (resid * inv[:, None] * norm_gain).astype(jnp.bfloat16).reshape(tok, groups_here, cblock)
    )
    gate_pre = jnp.einsum("tgc,gce->tge", normed, w_gate, preferred_element_type=jnp.float32)
    up_val = jnp.einsum("tgc,gce->tge", normed, w_up, preferred_element_type=jnp.float32)
    d_hidden = jnp.einsum(
        "tgc,gec->tge",
        cotangent.reshape(tok, groups_here, cblock),
        w_down,
        preferred_element_type=jnp.float32,
    )
    sig = jax.nn.sigmoid(gate_pre)
    d_up = (d_hidden * gate_pre * sig).astype(jnp.bfloat16)
    d_gate = (d_hidden * up_val * sig * (1.0 + gate_pre * (1.0 - sig))).astype(jnp.bfloat16)
    d_normed = jnp.einsum("tge,gce->tgc", d_gate, w_gate, preferred_element_type=jnp.float32)
    d_normed = d_normed + jnp.einsum("tge,gce->tgc", d_up, w_up, preferred_element_type=jnp.float32)
    scaled = norm_gain * d_normed.reshape(tok, width)
    inner = hid_sum(jnp.sum(resid * scaled, axis=-1))
    d_resid = (
        cotangent.astype(jnp.float32)
        + inv[:, None] * scaled
        - resid * (inv**3 * inner / D)[:, None]
    )
    d_mixed = (d_resid * tok_f).astype(jnp.bfloat16)
    grads_self = [None] * sections
    grads_cross = [None] * sections
    back = d_mixed
    for section in range(sections - 1, -1, -1):
        back_f = back.astype(jnp.float32)
        grads_self[section] = jnp.sum(back_f * states[section].astype(jnp.float32), axis=-1)
        grads_cross[section] = jnp.sum(back_f * mates[section].astype(jnp.float32), axis=-1)
        sent = (coef_cross[section][:, None] * back_f).astype(jnp.bfloat16)
        received = from_partner(sent, "seq", section)
        back = (coef_self[section][:, None] * back_f + received.astype(jnp.float32)).astype(
            jnp.bfloat16
        )
    direct = d_resid * (1.0 + mixed_f)
    return back, direct, jnp.stack(grads_self), jnp.stack(grads_cross)


def body(tokens, cotangent, blocks, coef_self, coef_cross, norm_gain, w_gate, w_up, w_down):
    tok, width = tokens.shape
    nblk = blocks.shape[0]
    blen = blocks.shape[1]
    tok_blocks = tokens.reshape(nblk, blen, width)
    local = jnp.einsum("kij,kjd->kid", blocks, tok_blocks, preferred_element_type=jnp.float32)
    local = local.astype(jnp.bfloat16).reshape(tok, width)
    chunks = CHUNKS if tok % CHUNKS == 0 else 1
    rows = tok // chunks
    results = []
    for chunk in range(chunks):
        rs = slice(chunk * rows, (chunk + 1) * rows)
        results.append(
            chain(
                local[rs], tokens[rs], cotangent[rs], coef_self[:, rs], coef_cross[:, rs],
                norm_gain, w_gate, w_up, w_down,
            )
        )
    back = jnp.concatenate([r[0] for r in results], axis=0)
    direct = jnp.concatenate([r[1] for r in results], axis=0)
    part_self = jnp.concatenate([r[2] for r in results], axis=1)
    part_cross = jnp.concatenate([r[3] for r in results], axis=1)
    back_blocks = back.reshape(nblk, blen, width)
    part_blocks = jnp.einsum(
        "kid,kjd->kij", back_blocks, tok_blocks, preferred_element_type=jnp.float32
    )
    from_blocks = jnp.einsum(
        "kij,kid->kjd", blocks, back_blocks, preferred_element_type=jnp.float32
    ).reshape(tok, width)
    grad_self, grad_cross, grad_blocks = jax.tree.map(hid_sum, (part_self, part_cross, part_blocks))
    grad_x = (direct + from_blocks).astype(jnp.bfloat16)
    return (grad_x, grad_self, grad_cross, grad_blocks)


def solution(mesh):
    return jax.shard_map(
        body,
        mesh=mesh,
        in_specs=(
            P(("groups", "seq"), "hid"),
            P(("groups", "seq"), "hid"),
            P("seq", None, None),
            P(None, "seq"),
            P(None, "seq"),
            P("hid"),
            P("hid", None, None),
            P("hid", None, None),
            P("hid", None, None),
        ),
        out_specs=(
            P(("groups", "seq"), "hid"),
            P(None, ("groups", "seq")),
            P(None, ("groups", "seq")),
            P(("groups", "seq"), None, None),
        ),
        check_vma=False,
    )
```

```python
import jax
import jax.numpy as jnp
from jax import lax
from jax.sharding import PartitionSpec as P

D = 2048
CHUNKS = 2


def from_partner(value, axis, distance):
    mask = 2**distance
    pairs = [(source, source ^ mask) for source in range(lax.axis_size(axis))]
    return lax.ppermute(value, axis, pairs)


def hid_sum(value):
    size = lax.axis_size("hid")
    total = value
    for shift in range(1, size):
        pairs = [(source, (source + shift) % size) for source in range(size)]
        total = total + lax.ppermute(value, "hid", pairs)
    return total


def tie(value, after):
    if after is None:
        return value
    return lax.optimization_barrier((value, after))[0]


def body(tokens, cotangent, blocks, coef_self, coef_cross, norm_gain, w_gate, w_up, w_down):
    tok, width = tokens.shape
    sections = coef_self.shape[0]
    nblk = blocks.shape[0]
    blen = blocks.shape[1]
    groups_here = w_gate.shape[0]
    cblock = w_gate.shape[1]
    tok_blocks = tokens.reshape(nblk, blen, width)
    local = jnp.einsum("kij,kjd->kid", blocks, tok_blocks, preferred_element_type=jnp.float32)
    local = local.astype(jnp.bfloat16).reshape(tok, width)
    chunks = CHUNKS if tok % CHUNKS == 0 else 1
    rows = tok // chunks
    spans = [slice(chunk * rows, (chunk + 1) * rows) for chunk in range(chunks)]

    states = [[None] * sections for _ in spans]
    mates = [[None] * sections for _ in spans]
    current = [local[rs] for rs in spans]
    for section in range(sections):
        previous = None
        for chunk, rs in enumerate(spans):
            value = tie(current[chunk], previous)
            mate = from_partner(value, "seq", section)
            previous = mate
            states[chunk][section] = value
            mates[chunk][section] = mate
            current[chunk] = (
                coef_self[section, rs][:, None] * value.astype(jnp.float32)
                + coef_cross[section, rs][:, None] * mate.astype(jnp.float32)
            ).astype(jnp.bfloat16)

    backs = []
    directs = []
    tok_fs = []
    for chunk, rs in enumerate(spans):
        tok_f = tokens[rs].astype(jnp.float32)
        cot = cotangent[rs]
        mixed_f = current[chunk].astype(jnp.float32)
        resid = tok_f + tok_f * mixed_f
        square = hid_sum(jnp.sum(resid * resid, axis=-1))
        inv = lax.rsqrt(square / D + 1e-06)
        normed = (
            (resid * inv[:, None] * norm_gain).astype(jnp.bfloat16).reshape(rows, groups_here, cblock)
        )
        gate_pre = jnp.einsum("tgc,gce->tge", normed, w_gate, preferred_element_type=jnp.float32)
        up_val = jnp.einsum("tgc,gce->tge", normed, w_up, preferred_element_type=jnp.float32)
        d_hidden = jnp.einsum(
            "tgc,gec->tge",
            cot.reshape(rows, groups_here, cblock),
            w_down,
            preferred_element_type=jnp.float32,
        )
        sig = jax.nn.sigmoid(gate_pre)
        d_up = (d_hidden * gate_pre * sig).astype(jnp.bfloat16)
        d_gate = (d_hidden * up_val * sig * (1.0 + gate_pre * (1.0 - sig))).astype(jnp.bfloat16)
        d_normed = jnp.einsum("tge,gce->tgc", d_gate, w_gate, preferred_element_type=jnp.float32)
        d_normed = d_normed + jnp.einsum(
            "tge,gce->tgc", d_up, w_up, preferred_element_type=jnp.float32
        )
        scaled = norm_gain * d_normed.reshape(rows, width)
        inner = hid_sum(jnp.sum(resid * scaled, axis=-1))
        d_resid = (
            cot.astype(jnp.float32)
            + inv[:, None] * scaled
            - resid * (inv**3 * inner / D)[:, None]
        )
        backs.append((d_resid * tok_f).astype(jnp.bfloat16))
        directs.append(d_resid * (1.0 + mixed_f))

    grads_self = [[None] * sections for _ in spans]
    grads_cross = [[None] * sections for _ in spans]
    for section in range(sections - 1, -1, -1):
        previous = None
        for chunk, rs in enumerate(spans):
            back_f = backs[chunk].astype(jnp.float32)
            grads_self[chunk][section] = jnp.sum(
                back_f * states[chunk][section].astype(jnp.float32), axis=-1
            )
            grads_cross[chunk][section] = jnp.sum(
                back_f * mates[chunk][section].astype(jnp.float32), axis=-1
            )
            sent = tie((coef_cross[section, rs][:, None] * back_f).astype(jnp.bfloat16), previous)
            received = from_partner(sent, "seq", section)
            previous = received
            backs[chunk] = (
                coef_self[section, rs][:, None] * back_f + received.astype(jnp.float32)
            ).astype(jnp.bfloat16)

    back = jnp.concatenate(backs, axis=0)
    direct = jnp.concatenate(directs, axis=0)
    part_self = jnp.concatenate([jnp.stack(g) for g in grads_self], axis=1)
    part_cross = jnp.concatenate([jnp.stack(g) for g in grads_cross], axis=1)
    back_blocks = back.reshape(nblk, blen, width)
    part_blocks = jnp.einsum(
        "kid,kjd->kij", back_blocks, tok_blocks, preferred_element_type=jnp.float32
    )
    from_blocks = jnp.einsum(
        "kij,kid->kjd", blocks, back_blocks, preferred_element_type=jnp.float32
    ).reshape(tok, width)
    grad_self, grad_cross, grad_blocks = jax.tree.map(hid_sum, (part_self, part_cross, part_blocks))
    grad_x = (direct + from_blocks).astype(jnp.bfloat16)
    return (grad_x, grad_self, grad_cross, grad_blocks)


def solution(mesh):
    return jax.shard_map(
        body,
        mesh=mesh,
        in_specs=(
            P(("groups", "seq"), "hid"),
            P(("groups", "seq"), "hid"),
            P("seq", None, None),
            P(None, "seq"),
            P(None, "seq"),
            P("hid"),
            P("hid", None, None),
            P("hid", None, None),
            P("hid", None, None),
        ),
        out_specs=(
            P(("groups", "seq"), "hid"),
            P(None, ("groups", "seq")),
            P(None, ("groups", "seq")),
            P(("groups", "seq"), None, None),
        ),
        check_vma=False,
    )
```

```python
import jax
import jax.numpy as jnp
from jax import lax
from jax.sharding import PartitionSpec as P
from jax.experimental import pallas as pl

D = 2048
CHUNKS = 2


def from_partner(value, axis, distance):
    mask = 2**distance
    pairs = [(source, source ^ mask) for source in range(lax.axis_size(axis))]
    return lax.ppermute(value, axis, pairs)


def ffn_kernel(normed_ref, cot_ref, wg_ref, wu_ref, wd_ref, out_ref):
    normed = normed_ref[...]
    w_gate = wg_ref[0]
    w_up = wu_ref[0]
    contract_last = (((1,), (1,)), ((), ()))
    gate_pre = jnp.dot(normed, w_gate, preferred_element_type=jnp.float32)
    up_val = jnp.dot(normed, w_up, preferred_element_type=jnp.float32)
    d_hidden = lax.dot_general(
        cot_ref[...], wd_ref[0], contract_last, preferred_element_type=jnp.float32
    )
    sig = 1.0 / (1.0 + jnp.exp(-gate_pre))
    d_up = (d_hidden * gate_pre * sig).astype(jnp.bfloat16)
    d_gate = (d_hidden * up_val * sig * (1.0 + gate_pre * (1.0 - sig))).astype(jnp.bfloat16)
    out_ref[...] = lax.dot_general(
        d_gate, w_gate, contract_last, preferred_element_type=jnp.float32
    ) + lax.dot_general(d_up, w_up, contract_last, preferred_element_type=jnp.float32)


def ffn_grad(normed, cotangent, w_gate, w_up, w_down):
    tok, width = normed.shape
    groups_here, cblock, hidden = w_gate.shape
    act = pl.BlockSpec((tok, cblock), lambda g: (0, g))
    return pl.pallas_call(
        ffn_kernel,
        grid=(groups_here,),
        in_specs=[
            act,
            act,
            pl.BlockSpec((1, cblock, hidden), lambda g: (g, 0, 0)),
            pl.BlockSpec((1, cblock, hidden), lambda g: (g, 0, 0)),
            pl.BlockSpec((1, hidden, cblock), lambda g: (g, 0, 0)),
        ],
        out_specs=act,
        out_shape=jax.ShapeDtypeStruct((tok, width), jnp.float32),
    )(normed, cotangent, w_gate, w_up, w_down)


def hid_sum(value):
    size = lax.axis_size("hid")
    total = value
    for shift in range(1, size):
        pairs = [(source, (source + shift) % size) for source in range(size)]
        total = total + lax.ppermute(value, "hid", pairs)
    return total


def chain(local, tokens, cotangent, coef_self, coef_cross, norm_gain, w_gate, w_up, w_down):
    tok, width = tokens.shape
    sections = coef_self.shape[0]
    groups_here = w_gate.shape[0]
    cblock = w_gate.shape[1]
    states = []
    mates = []
    current = local
    for section in range(sections):
        mate = from_partner(current, "seq", section)
        states.append(current)
        mates.append(mate)
        current = (
            coef_self[section][:, None] * current.astype(jnp.float32)
            + coef_cross[section][:, None] * mate.astype(jnp.float32)
        ).astype(jnp.bfloat16)
    tok_f = tokens.astype(jnp.float32)
    mixed_f = current.astype(jnp.float32)
    resid = tok_f + tok_f * mixed_f
    square = hid_sum(jnp.sum(resid * resid, axis=-1))
    inv = lax.rsqrt(square / D + 1e-06)
    normed = (resid * inv[:, None] * norm_gain).astype(jnp.bfloat16)
    d_normed = ffn_grad(normed, cotangent, w_gate, w_up, w_down)
    scaled = norm_gain * d_normed
    inner = hid_sum(jnp.sum(resid * scaled, axis=-1))
    d_resid = (
        cotangent.astype(jnp.float32)
        + inv[:, None] * scaled
        - resid * (inv**3 * inner / D)[:, None]
    )
    d_mixed = (d_resid * tok_f).astype(jnp.bfloat16)
    grads_self = [None] * sections
    grads_cross = [None] * sections
    back = d_mixed
    for section in range(sections - 1, -1, -1):
        back_f = back.astype(jnp.float32)
        grads_self[section] = jnp.sum(back_f * states[section].astype(jnp.float32), axis=-1)
        grads_cross[section] = jnp.sum(back_f * mates[section].astype(jnp.float32), axis=-1)
        sent = (coef_cross[section][:, None] * back_f).astype(jnp.bfloat16)
        received = from_partner(sent, "seq", section)
        back = (coef_self[section][:, None] * back_f + received.astype(jnp.float32)).astype(
            jnp.bfloat16
        )
    direct = d_resid * (1.0 + mixed_f)
    return back, direct, jnp.stack(grads_self), jnp.stack(grads_cross)


def body(tokens, cotangent, blocks, coef_self, coef_cross, norm_gain, w_gate, w_up, w_down):
    tok, width = tokens.shape
    nblk = blocks.shape[0]
    blen = blocks.shape[1]
    tok_blocks = tokens.reshape(nblk, blen, width)
    local = jnp.einsum("kij,kjd->kid", blocks, tok_blocks, preferred_element_type=jnp.float32)
    local = local.astype(jnp.bfloat16).reshape(tok, width)
    chunks = CHUNKS if tok % CHUNKS == 0 else 1
    rows = tok // chunks
    results = []
    for chunk in range(chunks):
        rs = slice(chunk * rows, (chunk + 1) * rows)
        results.append(
            chain(
                local[rs], tokens[rs], cotangent[rs], coef_self[:, rs], coef_cross[:, rs],
                norm_gain, w_gate, w_up, w_down,
            )
        )
    back = jnp.concatenate([r[0] for r in results], axis=0)
    direct = jnp.concatenate([r[1] for r in results], axis=0)
    part_self = jnp.concatenate([r[2] for r in results], axis=1)
    part_cross = jnp.concatenate([r[3] for r in results], axis=1)
    back_blocks = back.reshape(nblk, blen, width)
    part_blocks = jnp.einsum(
        "kid,kjd->kij", back_blocks, tok_blocks, preferred_element_type=jnp.float32
    )
    from_blocks = jnp.einsum(
        "kij,kid->kjd", blocks, back_blocks, preferred_element_type=jnp.float32
    ).reshape(tok, width)
    grad_self, grad_cross, grad_blocks = jax.tree.map(hid_sum, (part_self, part_cross, part_blocks))
    grad_x = (direct + from_blocks).astype(jnp.bfloat16)
    return (grad_x, grad_self, grad_cross, grad_blocks)


def solution(mesh):
    return jax.shard_map(
        body,
        mesh=mesh,
        in_specs=(
            P(("groups", "seq"), "hid"),
            P(("groups", "seq"), "hid"),
            P("seq", None, None),
            P(None, "seq"),
            P(None, "seq"),
            P("hid"),
            P("hid", None, None),
            P("hid", None, None),
            P("hid", None, None),
        ),
        out_specs=(
            P(("groups", "seq"), "hid"),
            P(None, ("groups", "seq")),
            P(None, ("groups", "seq")),
            P(("groups", "seq"), None, None),
        ),
        check_vma=False,
    )
```

```python
import jax
import jax.numpy as jnp
from jax import lax
from jax.sharding import PartitionSpec as P
from jax.experimental import pallas as pl

D = 2048


def from_partner(value, axis, distance):
    mask = 2**distance
    pairs = [(source, source ^ mask) for source in range(lax.axis_size(axis))]
    return lax.ppermute(value, axis, pairs)


def ffn_kernel(normed_ref, cot_ref, wg_ref, wu_ref, wd_ref, out_ref):
    cblock = wg_ref.shape[1]
    contract_last = (((1,), (1,)), ((), ()))
    for group in range(wg_ref.shape[0]):
        cols = slice(group * cblock, (group + 1) * cblock)
        normed = normed_ref[:, cols]
        w_gate = wg_ref[group]
        w_up = wu_ref[group]
        gate_pre = jnp.dot(normed, w_gate, preferred_element_type=jnp.float32)
        up_val = jnp.dot(normed, w_up, preferred_element_type=jnp.float32)
        d_hidden = lax.dot_general(
            cot_ref[:, cols], wd_ref[group], contract_last, preferred_element_type=jnp.float32
        )
        sig = 1.0 / (1.0 + jnp.exp(-gate_pre))
        d_up = (d_hidden * gate_pre * sig).astype(jnp.bfloat16)
        d_gate = (d_hidden * up_val * sig * (1.0 + gate_pre * (1.0 - sig))).astype(jnp.bfloat16)
        out_ref[:, cols] = lax.dot_general(
            d_gate, w_gate, contract_last, preferred_element_type=jnp.float32
        ) + lax.dot_general(d_up, w_up, contract_last, preferred_element_type=jnp.float32)


def ffn_grad(normed, cotangent, w_gate, w_up, w_down, per_step=4):
    tok, width = normed.shape
    groups_here, cblock, hidden = w_gate.shape
    if groups_here % per_step:
        per_step = 1
    act = pl.BlockSpec((tok, cblock * per_step), lambda g: (0, g))
    return pl.pallas_call(
        ffn_kernel,
        grid=(groups_here // per_step,),
        in_specs=[
            act,
            act,
            pl.BlockSpec((per_step, cblock, hidden), lambda g: (g, 0, 0)),
            pl.BlockSpec((per_step, cblock, hidden), lambda g: (g, 0, 0)),
            pl.BlockSpec((per_step, hidden, cblock), lambda g: (g, 0, 0)),
        ],
        out_specs=act,
        out_shape=jax.ShapeDtypeStruct((tok, width), jnp.float32),
    )(normed, cotangent, w_gate, w_up, w_down)


def hid_sum(value):
    size = lax.axis_size("hid")
    total = value
    for shift in range(1, size):
        pairs = [(source, (source + shift) % size) for source in range(size)]
        total = total + lax.ppermute(value, "hid", pairs)
    return total


def body(tokens, cotangent, blocks, coef_self, coef_cross, norm_gain, w_gate, w_up, w_down):
    tok, width = tokens.shape
    sections = lax.axis_size("seq").bit_length() - 1
    nblk = blocks.shape[0]
    blen = blocks.shape[1]
    tok_blocks = tokens.reshape(nblk, blen, width)
    local = jnp.einsum("kij,kjd->kid", blocks, tok_blocks, preferred_element_type=jnp.float32)
    local = local.astype(jnp.bfloat16).reshape(tok, width)
    states = []
    mates = []
    current = local
    for section in range(sections):
        mate = from_partner(current, "seq", section)
        states.append(current)
        mates.append(mate)
        current = (
            coef_self[section][:, None] * current.astype(jnp.float32)
            + coef_cross[section][:, None] * mate.astype(jnp.float32)
        ).astype(jnp.bfloat16)
    tok_f = tokens.astype(jnp.float32)
    mixed_f = current.astype(jnp.float32)
    resid = tok_f + tok_f * mixed_f
    square = hid_sum(jnp.sum(resid * resid, axis=-1))
    inv = lax.rsqrt(square / D + 1e-06)
    normed = (resid * inv[:, None] * norm_gain).astype(jnp.bfloat16)
    d_normed = ffn_grad(normed, cotangent, w_gate, w_up, w_down)
    scaled = norm_gain * d_normed
    inner = hid_sum(jnp.sum(resid * scaled, axis=-1))
    d_resid = (
        cotangent.astype(jnp.float32)
        + inv[:, None] * scaled
        - resid * (inv**3 * inner / D)[:, None]
    )
    d_mixed = (d_resid * tok_f).astype(jnp.bfloat16)
    grads_self = [None] * sections
    grads_cross = [None] * sections
    back = d_mixed
    for section in range(sections - 1, -1, -1):
        back_f = back.astype(jnp.float32)
        grads_self[section] = jnp.sum(back_f * states[section].astype(jnp.float32), axis=-1)
        grads_cross[section] = jnp.sum(back_f * mates[section].astype(jnp.float32), axis=-1)
        sent = (coef_cross[section][:, None] * back_f).astype(jnp.bfloat16)
        received = from_partner(sent, "seq", section)
        back = (coef_self[section][:, None] * back_f + received.astype(jnp.float32)).astype(
            jnp.bfloat16
        )
    part_self = jnp.stack(grads_self)
    part_cross = jnp.stack(grads_cross)
    back_blocks = back.reshape(nblk, blen, width)
    part_blocks = jnp.einsum(
        "kid,kjd->kij", back_blocks, tok_blocks, preferred_element_type=jnp.float32
    )
    from_blocks = jnp.einsum(
        "kij,kid->kjd", blocks, back_blocks, preferred_element_type=jnp.float32
    ).reshape(tok, width)
    grad_self, grad_cross, grad_blocks = jax.tree.map(hid_sum, (part_self, part_cross, part_blocks))
    grad_x = (d_resid * (1.0 + mixed_f) + from_blocks).astype(jnp.bfloat16)
    return (grad_x, grad_self, grad_cross, grad_blocks)


def solution(mesh):
    return jax.shard_map(
        body,
        mesh=mesh,
        in_specs=(
            P(("groups", "seq"), "hid"),
            P(("groups", "seq"), "hid"),
            P("seq", None, None),
            P(None, "seq"),
            P(None, "seq"),
            P("hid"),
            P("hid", None, None),
            P("hid", None, None),
            P("hid", None, None),
        ),
        out_specs=(
            P(("groups", "seq"), "hid"),
            P(None, ("groups", "seq")),
            P(None, ("groups", "seq")),
            P(("groups", "seq"), None, None),
        ),
        check_vma=False,
    )
```

```python
import jax
import jax.numpy as jnp
from jax import lax
from jax.sharding import PartitionSpec as P
from jax.experimental import pallas as pl

D = 2048
CHUNKS = 2


def from_partner(value, axis, distance):
    mask = 2**distance
    pairs = [(source, source ^ mask) for source in range(lax.axis_size(axis))]
    return lax.ppermute(value, axis, pairs)


def ffn_kernel(normed_ref, cot_ref, wg_ref, wu_ref, wd_ref, out_ref):
    cblock = wg_ref.shape[1]
    contract_last = (((1,), (1,)), ((), ()))
    for group in range(wg_ref.shape[0]):
        cols = slice(group * cblock, (group + 1) * cblock)
        normed = normed_ref[:, cols]
        w_gate = wg_ref[group]
        w_up = wu_ref[group]
        gate_pre = jnp.dot(normed, w_gate, preferred_element_type=jnp.float32)
        up_val = jnp.dot(normed, w_up, preferred_element_type=jnp.float32)
        d_hidden = lax.dot_general(
            cot_ref[:, cols], wd_ref[group], contract_last, preferred_element_type=jnp.float32
        )
        sig = 1.0 / (1.0 + jnp.exp(-gate_pre))
        d_up = (d_hidden * gate_pre * sig).astype(jnp.bfloat16)
        d_gate = (d_hidden * up_val * sig * (1.0 + gate_pre * (1.0 - sig))).astype(jnp.bfloat16)
        out_ref[:, cols] = lax.dot_general(
            d_gate, w_gate, contract_last, preferred_element_type=jnp.float32
        ) + lax.dot_general(d_up, w_up, contract_last, preferred_element_type=jnp.float32)


def ffn_grad(normed, cotangent, w_gate, w_up, w_down, per_step=4):
    tok, width = normed.shape
    groups_here, cblock, hidden = w_gate.shape
    if groups_here % per_step:
        per_step = 1
    act = pl.BlockSpec((tok, cblock * per_step), lambda g: (0, g))
    return pl.pallas_call(
        ffn_kernel,
        grid=(groups_here // per_step,),
        in_specs=[
            act,
            act,
            pl.BlockSpec((per_step, cblock, hidden), lambda g: (g, 0, 0)),
            pl.BlockSpec((per_step, cblock, hidden), lambda g: (g, 0, 0)),
            pl.BlockSpec((per_step, hidden, cblock), lambda g: (g, 0, 0)),
        ],
        out_specs=act,
        out_shape=jax.ShapeDtypeStruct((tok, width), jnp.float32),
    )(normed, cotangent, w_gate, w_up, w_down)


def hid_sum(value):
    size = lax.axis_size("hid")
    total = value
    for shift in range(1, size):
        pairs = [(source, (source + shift) % size) for source in range(size)]
        total = total + lax.ppermute(value, "hid", pairs)
    return total


def body(tokens, cotangent, blocks, coef_self, coef_cross, norm_gain, w_gate, w_up, w_down):
    tok, width = tokens.shape
    sections = lax.axis_size("seq").bit_length() - 1
    nblk = blocks.shape[0]
    blen = blocks.shape[1]
    tok_blocks = tokens.reshape(nblk, blen, width)
    local = jnp.einsum("kij,kjd->kid", blocks, tok_blocks, preferred_element_type=jnp.float32)
    local = local.astype(jnp.bfloat16).reshape(tok, width)
    chunks = CHUNKS if tok % CHUNKS == 0 else 1
    rows = tok // chunks
    spans = [slice(chunk * rows, (chunk + 1) * rows) for chunk in range(chunks)]
    states = [[None] * sections for _ in spans]
    mates = [[None] * sections for _ in spans]
    pieces = [local[rs] for rs in spans]
    for section in range(sections):
        for chunk, rs in enumerate(spans):
            value = pieces[chunk]
            mate = from_partner(value, "seq", section)
            states[chunk][section] = value
            mates[chunk][section] = mate
            pieces[chunk] = (
                coef_self[section, rs][:, None] * value.astype(jnp.float32)
                + coef_cross[section, rs][:, None] * mate.astype(jnp.float32)
            ).astype(jnp.bfloat16)
    current = jnp.concatenate(pieces, axis=0)
    tok_f = tokens.astype(jnp.float32)
    mixed_f = current.astype(jnp.float32)
    resid = tok_f + tok_f * mixed_f
    square = hid_sum(jnp.sum(resid * resid, axis=-1))
    inv = lax.rsqrt(square / D + 1e-06)
    normed = (resid * inv[:, None] * norm_gain).astype(jnp.bfloat16)
    d_normed = ffn_grad(normed, cotangent, w_gate, w_up, w_down)
    scaled = norm_gain * d_normed
    inner = hid_sum(jnp.sum(resid * scaled, axis=-1))
    d_resid = (
        cotangent.astype(jnp.float32)
        + inv[:, None] * scaled
        - resid * (inv**3 * inner / D)[:, None]
    )
    d_mixed = (d_resid * tok_f).astype(jnp.bfloat16)
    grads_self = [[None] * sections for _ in spans]
    grads_cross = [[None] * sections for _ in spans]
    backs = [d_mixed[rs] for rs in spans]
    for section in range(sections - 1, -1, -1):
        for chunk, rs in enumerate(spans):
            back_f = backs[chunk].astype(jnp.float32)
            grads_self[chunk][section] = jnp.sum(
                back_f * states[chunk][section].astype(jnp.float32), axis=-1
            )
            grads_cross[chunk][section] = jnp.sum(
                back_f * mates[chunk][section].astype(jnp.float32), axis=-1
            )
            sent = (coef_cross[section, rs][:, None] * back_f).astype(jnp.bfloat16)
            received = from_partner(sent, "seq", section)
            backs[chunk] = (
                coef_self[section, rs][:, None] * back_f + received.astype(jnp.float32)
            ).astype(jnp.bfloat16)
    back = jnp.concatenate(backs, axis=0)
    part_self = jnp.concatenate([jnp.stack(g) for g in grads_self], axis=1)
    part_cross = jnp.concatenate([jnp.stack(g) for g in grads_cross], axis=1)
    back_blocks = back.reshape(nblk, blen, width)
    part_blocks = jnp.einsum(
        "kid,kjd->kij", back_blocks, tok_blocks, preferred_element_type=jnp.float32
    )
    from_blocks = jnp.einsum(
        "kij,kid->kjd", blocks, back_blocks, preferred_element_type=jnp.float32
    ).reshape(tok, width)
    grad_self, grad_cross, grad_blocks = jax.tree.map(hid_sum, (part_self, part_cross, part_blocks))
    grad_x = (d_resid * (1.0 + mixed_f) + from_blocks).astype(jnp.bfloat16)
    return (grad_x, grad_self, grad_cross, grad_blocks)


def solution(mesh):
    return jax.shard_map(
        body,
        mesh=mesh,
        in_specs=(
            P(("groups", "seq"), "hid"),
            P(("groups", "seq"), "hid"),
            P("seq", None, None),
            P(None, "seq"),
            P(None, "seq"),
            P("hid"),
            P("hid", None, None),
            P("hid", None, None),
            P("hid", None, None),
        ),
        out_specs=(
            P(("groups", "seq"), "hid"),
            P(None, ("groups", "seq")),
            P(None, ("groups", "seq")),
            P(("groups", "seq"), None, None),
        ),
        check_vma=False,
    )
```

```python
import jax
import jax.numpy as jnp
from jax import lax
from jax.sharding import PartitionSpec as P
from jax.experimental import pallas as pl

D = 2048
CHUNKS = 4


def from_partner(value, axis, distance):
    mask = 2**distance
    pairs = [(source, source ^ mask) for source in range(lax.axis_size(axis))]
    return lax.ppermute(value, axis, pairs)


def ffn_kernel(normed_ref, cot_ref, wg_ref, wu_ref, wd_ref, out_ref):
    cblock = wg_ref.shape[1]
    contract_last = (((1,), (1,)), ((), ()))
    for group in range(wg_ref.shape[0]):
        cols = slice(group * cblock, (group + 1) * cblock)
        normed = normed_ref[:, cols]
        w_gate = wg_ref[group]
        w_up = wu_ref[group]
        gate_pre = jnp.dot(normed, w_gate, preferred_element_type=jnp.float32)
        up_val = jnp.dot(normed, w_up, preferred_element_type=jnp.float32)
        d_hidden = lax.dot_general(
            cot_ref[:, cols], wd_ref[group], contract_last, preferred_element_type=jnp.float32
        )
        sig = 1.0 / (1.0 + jnp.exp(-gate_pre))
        d_up = (d_hidden * gate_pre * sig).astype(jnp.bfloat16)
        d_gate = (d_hidden * up_val * sig * (1.0 + gate_pre * (1.0 - sig))).astype(jnp.bfloat16)
        out_ref[:, cols] = lax.dot_general(
            d_gate, w_gate, contract_last, preferred_element_type=jnp.float32
        ) + lax.dot_general(d_up, w_up, contract_last, preferred_element_type=jnp.float32)


def ffn_grad(normed, cotangent, w_gate, w_up, w_down, per_step=4):
    tok, width = normed.shape
    groups_here, cblock, hidden = w_gate.shape
    if groups_here % per_step:
        per_step = 1
    act = pl.BlockSpec((tok, cblock * per_step), lambda g: (0, g))
    return pl.pallas_call(
        ffn_kernel,
        grid=(groups_here // per_step,),
        in_specs=[
            act,
            act,
            pl.BlockSpec((per_step, cblock, hidden), lambda g: (g, 0, 0)),
            pl.BlockSpec((per_step, cblock, hidden), lambda g: (g, 0, 0)),
            pl.BlockSpec((per_step, hidden, cblock), lambda g: (g, 0, 0)),
        ],
        out_specs=act,
        out_shape=jax.ShapeDtypeStruct((tok, width), jnp.float32),
    )(normed, cotangent, w_gate, w_up, w_down)


def hid_sum(value):
    size = lax.axis_size("hid")
    total = value
    for shift in range(1, size):
        pairs = [(source, (source + shift) % size) for source in range(size)]
        total = total + lax.ppermute(value, "hid", pairs)
    return total


def body(tokens, cotangent, blocks, coef_self, coef_cross, norm_gain, w_gate, w_up, w_down):
    tok, width = tokens.shape
    sections = lax.axis_size("seq").bit_length() - 1
    nblk = blocks.shape[0]
    blen = blocks.shape[1]
    tok_blocks = tokens.reshape(nblk, blen, width)
    local = jnp.einsum("kij,kjd->kid", blocks, tok_blocks, preferred_element_type=jnp.float32)
    local = local.astype(jnp.bfloat16).reshape(tok, width)
    chunks = CHUNKS if tok % CHUNKS == 0 else 1
    rows = tok // chunks
    spans = [slice(chunk * rows, (chunk + 1) * rows) for chunk in range(chunks)]
    states = [[None] * sections for _ in spans]
    mates = [[None] * sections for _ in spans]
    pieces = [local[rs] for rs in spans]
    for section in range(sections):
        for chunk, rs in enumerate(spans):
            value = pieces[chunk]
            mate = from_partner(value, "seq", section)
            states[chunk][section] = value
            mates[chunk][section] = mate
            pieces[chunk] = (
                coef_self[section, rs][:, None] * value.astype(jnp.float32)
                + coef_cross[section, rs][:, None] * mate.astype(jnp.float32)
            ).astype(jnp.bfloat16)
    current = jnp.concatenate(pieces, axis=0)
    tok_f = tokens.astype(jnp.float32)
    mixed_f = current.astype(jnp.float32)
    resid = tok_f + tok_f * mixed_f
    square = hid_sum(jnp.sum(resid * resid, axis=-1))
    inv = lax.rsqrt(square / D + 1e-06)
    normed = (resid * inv[:, None] * norm_gain).astype(jnp.bfloat16)
    d_normed = ffn_grad(normed, cotangent, w_gate, w_up, w_down)
    scaled = norm_gain * d_normed
    inner = hid_sum(jnp.sum(resid * scaled, axis=-1))
    d_resid = (
        cotangent.astype(jnp.float32)
        + inv[:, None] * scaled
        - resid * (inv**3 * inner / D)[:, None]
    )
    d_mixed = (d_resid * tok_f).astype(jnp.bfloat16)
    grads_self = [[None] * sections for _ in spans]
    grads_cross = [[None] * sections for _ in spans]
    backs = [d_mixed[rs] for rs in spans]
    for section in range(sections - 1, -1, -1):
        for chunk, rs in enumerate(spans):
            back_f = backs[chunk].astype(jnp.float32)
            grads_self[chunk][section] = jnp.sum(
                back_f * states[chunk][section].astype(jnp.float32), axis=-1
            )
            grads_cross[chunk][section] = jnp.sum(
                back_f * mates[chunk][section].astype(jnp.float32), axis=-1
            )
            sent = (coef_cross[section, rs][:, None] * back_f).astype(jnp.bfloat16)
            received = from_partner(sent, "seq", section)
            backs[chunk] = (
                coef_self[section, rs][:, None] * back_f + received.astype(jnp.float32)
            ).astype(jnp.bfloat16)
    back = jnp.concatenate(backs, axis=0)
    part_self = jnp.concatenate([jnp.stack(g) for g in grads_self], axis=1)
    part_cross = jnp.concatenate([jnp.stack(g) for g in grads_cross], axis=1)
    back_blocks = back.reshape(nblk, blen, width)
    part_blocks = jnp.einsum(
        "kid,kjd->kij", back_blocks, tok_blocks, preferred_element_type=jnp.float32
    )
    from_blocks = jnp.einsum(
        "kij,kid->kjd", blocks, back_blocks, preferred_element_type=jnp.float32
    ).reshape(tok, width)
    grad_self, grad_cross, grad_blocks = jax.tree.map(hid_sum, (part_self, part_cross, part_blocks))
    grad_x = (d_resid * (1.0 + mixed_f) + from_blocks).astype(jnp.bfloat16)
    return (grad_x, grad_self, grad_cross, grad_blocks)


def solution(mesh):
    return jax.shard_map(
        body,
        mesh=mesh,
        in_specs=(
            P(("groups", "seq"), "hid"),
            P(("groups", "seq"), "hid"),
            P("seq", None, None),
            P(None, "seq"),
            P(None, "seq"),
            P("hid"),
            P("hid", None, None),
            P("hid", None, None),
            P("hid", None, None),
        ),
        out_specs=(
            P(("groups", "seq"), "hid"),
            P(None, ("groups", "seq")),
            P(None, ("groups", "seq")),
            P(("groups", "seq"), None, None),
        ),
        check_vma=False,
    )
```

```python
import jax
import jax.numpy as jnp
from jax import lax
from jax.sharding import PartitionSpec as P
from jax.experimental import pallas as pl

D = 2048
CHUNKS = 2


def from_partner(value, axis, distance):
    mask = 2**distance
    pairs = [(source, source ^ mask) for source in range(lax.axis_size(axis))]
    return lax.ppermute(value, axis, pairs)


def ffn_kernel(tok_ref, mix_ref, inv_ref, gain_ref, cot_ref, wg_ref, wu_ref, wd_ref,
               scaled_ref, acc_ref):
    cblock = wg_ref.shape[1]
    contract_last = (((1,), (1,)), ((), ()))
    inv = inv_ref[...]
    acc = jnp.zeros(acc_ref.shape, jnp.float32)
    for group in range(wg_ref.shape[0]):
        cols = slice(group * cblock, (group + 1) * cblock)
        tok = tok_ref[:, cols].astype(jnp.float32)
        resid = tok + tok * mix_ref[:, cols].astype(jnp.float32)
        gain = gain_ref[:, cols]
        normed = (resid * inv * gain).astype(jnp.bfloat16)
        w_gate = wg_ref[group]
        w_up = wu_ref[group]
        gate_pre = jnp.dot(normed, w_gate, preferred_element_type=jnp.float32)
        up_val = jnp.dot(normed, w_up, preferred_element_type=jnp.float32)
        d_hidden = lax.dot_general(
            cot_ref[:, cols], wd_ref[group], contract_last, preferred_element_type=jnp.float32
        )
        sig = 1.0 / (1.0 + jnp.exp(-gate_pre))
        d_up = (d_hidden * gate_pre * sig).astype(jnp.bfloat16)
        d_gate = (d_hidden * up_val * sig * (1.0 + gate_pre * (1.0 - sig))).astype(jnp.bfloat16)
        d_normed = lax.dot_general(
            d_gate, w_gate, contract_last, preferred_element_type=jnp.float32
        ) + lax.dot_general(d_up, w_up, contract_last, preferred_element_type=jnp.float32)
        scaled = gain * d_normed
        scaled_ref[:, cols] = scaled
        acc = acc + resid * scaled

    @pl.when(pl.program_id(0) == 0)
    def _():
        acc_ref[...] = acc

    @pl.when(pl.program_id(0) > 0)
    def _():
        acc_ref[...] += acc


def ffn_grad(tokens, mixed, inv, norm_gain, cotangent, w_gate, w_up, w_down, per_step=4):
    tok, width = tokens.shape
    groups_here, cblock, hidden = w_gate.shape
    if groups_here % per_step:
        per_step = 1
    act = pl.BlockSpec((tok, cblock * per_step), lambda g: (0, g))
    return pl.pallas_call(
        ffn_kernel,
        grid=(groups_here // per_step,),
        in_specs=[
            act,
            act,
            pl.BlockSpec((tok, 1), lambda g: (0, 0)),
            pl.BlockSpec((1, cblock * per_step), lambda g: (0, g)),
            act,
            pl.BlockSpec((per_step, cblock, hidden), lambda g: (g, 0, 0)),
            pl.BlockSpec((per_step, cblock, hidden), lambda g: (g, 0, 0)),
            pl.BlockSpec((per_step, hidden, cblock), lambda g: (g, 0, 0)),
        ],
        out_specs=[act, pl.BlockSpec((tok, cblock), lambda g: (0, 0))],
        out_shape=[
            jax.ShapeDtypeStruct((tok, width), jnp.float32),
            jax.ShapeDtypeStruct((tok, cblock), jnp.float32),
        ],
    )(tokens, mixed, inv[:, None], norm_gain[None, :], cotangent, w_gate, w_up, w_down)


def hid_sum(value):
    size = lax.axis_size("hid")
    total = value
    for shift in range(1, size):
        pairs = [(source, (source + shift) % size) for source in range(size)]
        total = total + lax.ppermute(value, "hid", pairs)
    return total


def body(tokens, cotangent, blocks, coef_self, coef_cross, norm_gain, w_gate, w_up, w_down):
    tok, width = tokens.shape
    sections = lax.axis_size("seq").bit_length() - 1
    nblk = blocks.shape[0]
    blen = blocks.shape[1]
    tok_blocks = tokens.reshape(nblk, blen, width)
    local = jnp.einsum("kij,kjd->kid", blocks, tok_blocks, preferred_element_type=jnp.float32)
    local = local.astype(jnp.bfloat16).reshape(tok, width)
    chunks = CHUNKS if tok % CHUNKS == 0 else 1
    rows = tok // chunks
    spans = [slice(chunk * rows, (chunk + 1) * rows) for chunk in range(chunks)]
    states = [[None] * sections for _ in spans]
    mates = [[None] * sections for _ in spans]
    pieces = [local[rs] for rs in spans]
    for section in range(sections):
        for chunk, rs in enumerate(spans):
            value = pieces[chunk]
            mate = from_partner(value, "seq", section)
            states[chunk][section] = value
            mates[chunk][section] = mate
            pieces[chunk] = (
                coef_self[section, rs][:, None] * value.astype(jnp.float32)
                + coef_cross[section, rs][:, None] * mate.astype(jnp.float32)
            ).astype(jnp.bfloat16)
    current = jnp.concatenate(pieces, axis=0)
    tok_f = tokens.astype(jnp.float32)
    mixed_f = current.astype(jnp.float32)
    resid = tok_f + tok_f * mixed_f
    square = hid_sum(jnp.sum(resid * resid, axis=-1))
    inv = lax.rsqrt(square / D + 1e-06)
    scaled, lanes = ffn_grad(tokens, current, inv, norm_gain, cotangent, w_gate, w_up, w_down)
    inner = hid_sum(jnp.sum(lanes, axis=-1))
    d_resid = (
        cotangent.astype(jnp.float32)
        + inv[:, None] * scaled
        - resid * (inv**3 * inner / D)[:, None]
    )
    d_mixed = (d_resid * tok_f).astype(jnp.bfloat16)
    grads_self = [[None] * sections for _ in spans]
    grads_cross = [[None] * sections for _ in spans]
    backs = [d_mixed[rs] for rs in spans]
    for section in range(sections - 1, -1, -1):
        for chunk, rs in enumerate(spans):
            back_f = backs[chunk].astype(jnp.float32)
            grads_self[chunk][section] = jnp.sum(
                back_f * states[chunk][section].astype(jnp.float32), axis=-1
            )
            grads_cross[chunk][section] = jnp.sum(
                back_f * mates[chunk][section].astype(jnp.float32), axis=-1
            )
            sent = (coef_cross[section, rs][:, None] * back_f).astype(jnp.bfloat16)
            received = from_partner(sent, "seq", section)
            backs[chunk] = (
                coef_self[section, rs][:, None] * back_f + received.astype(jnp.float32)
            ).astype(jnp.bfloat16)
    back = jnp.concatenate(backs, axis=0)
    part_self = jnp.concatenate([jnp.stack(g) for g in grads_self], axis=1)
    part_cross = jnp.concatenate([jnp.stack(g) for g in grads_cross], axis=1)
    back_blocks = back.reshape(nblk, blen, width)
    part_blocks = jnp.einsum(
        "kid,kjd->kij", back_blocks, tok_blocks, preferred_element_type=jnp.float32
    )
    from_blocks = jnp.einsum(
        "kij,kid->kjd", blocks, back_blocks, preferred_element_type=jnp.float32
    ).reshape(tok, width)
    grad_self, grad_cross, grad_blocks = jax.tree.map(hid_sum, (part_self, part_cross, part_blocks))
    grad_x = (d_resid * (1.0 + mixed_f) + from_blocks).astype(jnp.bfloat16)
    return (grad_x, grad_self, grad_cross, grad_blocks)


def solution(mesh):
    return jax.shard_map(
        body,
        mesh=mesh,
        in_specs=(
            P(("groups", "seq"), "hid"),
            P(("groups", "seq"), "hid"),
            P("seq", None, None),
            P(None, "seq"),
            P(None, "seq"),
            P("hid"),
            P("hid", None, None),
            P("hid", None, None),
            P("hid", None, None),
        ),
        out_specs=(
            P(("groups", "seq"), "hid"),
            P(None, ("groups", "seq")),
            P(None, ("groups", "seq")),
            P(("groups", "seq"), None, None),
        ),
        check_vma=False,
    )
```

```python
import jax
import jax.numpy as jnp
from jax import lax
from jax.sharding import PartitionSpec as P
from jax.experimental import pallas as pl

D = 2048
CHUNKS = 2


def from_partner(value, axis, distance):
    mask = 2**distance
    pairs = [(source, source ^ mask) for source in range(lax.axis_size(axis))]
    return lax.ppermute(value, axis, pairs)


def ffn_kernel(normed_ref, cot_ref, wg_ref, wu_ref, wd_ref, out_ref):
    cblock = wg_ref.shape[1]
    contract_last = (((1,), (1,)), ((), ()))
    for group in range(wg_ref.shape[0]):
        cols = slice(group * cblock, (group + 1) * cblock)
        normed = normed_ref[:, cols]
        w_gate = wg_ref[group]
        w_up = wu_ref[group]
        gate_pre = jnp.dot(normed, w_gate, preferred_element_type=jnp.float32)
        up_val = jnp.dot(normed, w_up, preferred_element_type=jnp.float32)
        d_hidden = lax.dot_general(
            cot_ref[:, cols], wd_ref[group], contract_last, preferred_element_type=jnp.float32
        )
        sig = 1.0 / (1.0 + jnp.exp(-gate_pre))
        d_up = (d_hidden * gate_pre * sig).astype(jnp.bfloat16)
        d_gate = (d_hidden * up_val * sig * (1.0 + gate_pre * (1.0 - sig))).astype(jnp.bfloat16)
        out_ref[:, cols] = lax.dot_general(
            d_gate, w_gate, contract_last, preferred_element_type=jnp.float32
        ) + lax.dot_general(d_up, w_up, contract_last, preferred_element_type=jnp.float32)


def ffn_grad(normed, cotangent, w_gate, w_up, w_down, per_step=4):
    tok, width = normed.shape
    groups_here, cblock, hidden = w_gate.shape
    if groups_here % per_step:
        per_step = 1
    act = pl.BlockSpec((tok, cblock * per_step), lambda g: (0, g))
    return pl.pallas_call(
        ffn_kernel,
        grid=(groups_here // per_step,),
        in_specs=[
            act,
            act,
            pl.BlockSpec((per_step, cblock, hidden), lambda g: (g, 0, 0)),
            pl.BlockSpec((per_step, cblock, hidden), lambda g: (g, 0, 0)),
            pl.BlockSpec((per_step, hidden, cblock), lambda g: (g, 0, 0)),
        ],
        out_specs=act,
        out_shape=jax.ShapeDtypeStruct((tok, width), jnp.float32),
    )(normed, cotangent, w_gate, w_up, w_down)


def hid_sum(value):
    size = lax.axis_size("hid")
    total = value
    for shift in range(1, size):
        pairs = [(source, (source + shift) % size) for source in range(size)]
        total = total + lax.ppermute(value, "hid", pairs)
    return total


def body(tokens, cotangent, blocks, coef_self, coef_cross, norm_gain, w_gate, w_up, w_down):
    tok, width = tokens.shape
    sections = lax.axis_size("seq").bit_length() - 1
    nblk = blocks.shape[0]
    blen = blocks.shape[1]
    tok_blocks = tokens.reshape(nblk, blen, width)
    chunks = CHUNKS if tok % CHUNKS == 0 else 1
    rows = tok // chunks
    spans = [slice(chunk * rows, (chunk + 1) * rows) for chunk in range(chunks)]
    states = [[None] * sections for _ in spans]
    mates = [[None] * sections for _ in spans]
    if nblk == 1:
        pieces = [
            jnp.einsum(
                "kij,kjd->kid", blocks[:, rs], tok_blocks, preferred_element_type=jnp.float32
            ).astype(jnp.bfloat16).reshape(rows, width)
            for rs in spans
        ]
    else:
        local = jnp.einsum(
            "kij,kjd->kid", blocks, tok_blocks, preferred_element_type=jnp.float32
        ).astype(jnp.bfloat16).reshape(tok, width)
        pieces = [local[rs] for rs in spans]
    for section in range(sections):
        for chunk, rs in enumerate(spans):
            value = pieces[chunk]
            mate = from_partner(value, "seq", section)
            states[chunk][section] = value
            mates[chunk][section] = mate
            pieces[chunk] = (
                coef_self[section, rs][:, None] * value.astype(jnp.float32)
                + coef_cross[section, rs][:, None] * mate.astype(jnp.float32)
            ).astype(jnp.bfloat16)
    current = jnp.concatenate(pieces, axis=0)
    tok_f = tokens.astype(jnp.float32)
    mixed_f = current.astype(jnp.float32)
    resid = tok_f + tok_f * mixed_f
    square = hid_sum(jnp.sum(resid * resid, axis=-1))
    inv = lax.rsqrt(square / D + 1e-06)
    normed = (resid * inv[:, None] * norm_gain).astype(jnp.bfloat16)
    d_normed = ffn_grad(normed, cotangent, w_gate, w_up, w_down)
    scaled = norm_gain * d_normed
    inner = hid_sum(jnp.sum(resid * scaled, axis=-1))
    d_resid = (
        cotangent.astype(jnp.float32)
        + inv[:, None] * scaled
        - resid * (inv**3 * inner / D)[:, None]
    )
    d_mixed = (d_resid * tok_f).astype(jnp.bfloat16)
    grads_self = [[None] * sections for _ in spans]
    grads_cross = [[None] * sections for _ in spans]
    backs = [d_mixed[rs] for rs in spans]
    for section in range(sections - 1, -1, -1):
        for chunk, rs in enumerate(spans):
            back_f = backs[chunk].astype(jnp.float32)
            grads_self[chunk][section] = jnp.sum(
                back_f * states[chunk][section].astype(jnp.float32), axis=-1
            )
            grads_cross[chunk][section] = jnp.sum(
                back_f * mates[chunk][section].astype(jnp.float32), axis=-1
            )
            sent = (coef_cross[section, rs][:, None] * back_f).astype(jnp.bfloat16)
            received = from_partner(sent, "seq", section)
            backs[chunk] = (
                coef_self[section, rs][:, None] * back_f + received.astype(jnp.float32)
            ).astype(jnp.bfloat16)
    back = jnp.concatenate(backs, axis=0)
    part_self = jnp.concatenate([jnp.stack(g) for g in grads_self], axis=1)
    part_cross = jnp.concatenate([jnp.stack(g) for g in grads_cross], axis=1)
    back_blocks = back.reshape(nblk, blen, width)
    part_blocks = jnp.einsum(
        "kid,kjd->kij", back_blocks, tok_blocks, preferred_element_type=jnp.float32
    )
    from_blocks = jnp.einsum(
        "kij,kid->kjd", blocks, back_blocks, preferred_element_type=jnp.float32
    ).reshape(tok, width)
    grad_self, grad_cross, grad_blocks = jax.tree.map(hid_sum, (part_self, part_cross, part_blocks))
    grad_x = (d_resid * (1.0 + mixed_f) + from_blocks).astype(jnp.bfloat16)
    return (grad_x, grad_self, grad_cross, grad_blocks)


def solution(mesh):
    return jax.shard_map(
        body,
        mesh=mesh,
        in_specs=(
            P(("groups", "seq"), "hid"),
            P(("groups", "seq"), "hid"),
            P("seq", None, None),
            P(None, "seq"),
            P(None, "seq"),
            P("hid"),
            P("hid", None, None),
            P("hid", None, None),
            P("hid", None, None),
        ),
        out_specs=(
            P(("groups", "seq"), "hid"),
            P(None, ("groups", "seq")),
            P(None, ("groups", "seq")),
            P(("groups", "seq"), None, None),
        ),
        check_vma=False,
    )
```

```python
import jax
import jax.numpy as jnp
from jax import lax
from jax.sharding import PartitionSpec as P
from jax.experimental import pallas as pl

D = 2048
CHUNKS = 2


def from_partner(value, axis, distance):
    mask = 2**distance
    pairs = [(source, source ^ mask) for source in range(lax.axis_size(axis))]
    return lax.ppermute(value, axis, pairs)


def ffn_kernel(*refs):
    *mix_refs, tok_ref, inv_ref, gain_ref, cot_ref, wg_ref, wu_ref, wd_ref, scaled_ref, inner_ref = refs
    cblock = wg_ref.shape[1]
    contract_last = (((1,), (1,)), ((), ()))
    inv = inv_ref[...]
    acc = jnp.zeros((tok_ref.shape[0], cblock), jnp.float32)
    for group in range(wg_ref.shape[0]):
        cols = slice(group * cblock, (group + 1) * cblock)
        mixed = jnp.concatenate([ref[:, cols] for ref in mix_refs], axis=0)
        tok = tok_ref[:, cols].astype(jnp.float32)
        resid = tok + tok * mixed.astype(jnp.float32)
        gain = gain_ref[:, cols]
        normed = (resid * inv * gain).astype(jnp.bfloat16)
        w_gate = wg_ref[group]
        w_up = wu_ref[group]
        gate_pre = jnp.dot(normed, w_gate, preferred_element_type=jnp.float32)
        up_val = jnp.dot(normed, w_up, preferred_element_type=jnp.float32)
        d_hidden = lax.dot_general(
            cot_ref[:, cols], wd_ref[group], contract_last, preferred_element_type=jnp.float32
        )
        sig = 1.0 / (1.0 + jnp.exp(-gate_pre))
        d_up = (d_hidden * gate_pre * sig).astype(jnp.bfloat16)
        d_gate = (d_hidden * up_val * sig * (1.0 + gate_pre * (1.0 - sig))).astype(jnp.bfloat16)
        d_normed = lax.dot_general(
            d_gate, w_gate, contract_last, preferred_element_type=jnp.float32
        ) + lax.dot_general(d_up, w_up, contract_last, preferred_element_type=jnp.float32)
        scaled = gain * d_normed
        scaled_ref[:, cols] = scaled
        acc = acc + resid * scaled
    part = jnp.sum(acc, axis=1, keepdims=True)

    @pl.when(pl.program_id(0) == 0)
    def _():
        inner_ref[...] = part

    @pl.when(pl.program_id(0) > 0)
    def _():
        inner_ref[...] += part


def ffn_grad(pieces, tokens, inv, norm_gain, cotangent, w_gate, w_up, w_down, per_step=4):
    tok, width = tokens.shape
    groups_here, cblock, hidden = w_gate.shape
    if groups_here % per_step:
        per_step = 1
    cols = cblock * per_step
    act = pl.BlockSpec((tok, cols), lambda g: (0, g))
    piece_specs = [pl.BlockSpec((piece.shape[0], cols), lambda g: (0, g)) for piece in pieces]
    return pl.pallas_call(
        ffn_kernel,
        grid=(groups_here // per_step,),
        in_specs=piece_specs + [
            act,
            pl.BlockSpec((tok, 1), lambda g: (0, 0)),
            pl.BlockSpec((1, cols), lambda g: (0, g)),
            act,
            pl.BlockSpec((per_step, cblock, hidden), lambda g: (g, 0, 0)),
            pl.BlockSpec((per_step, cblock, hidden), lambda g: (g, 0, 0)),
            pl.BlockSpec((per_step, hidden, cblock), lambda g: (g, 0, 0)),
        ],
        out_specs=[act, pl.BlockSpec((tok, 1), lambda g: (0, 0))],
        out_shape=[
            jax.ShapeDtypeStruct((tok, width), jnp.float32),
            jax.ShapeDtypeStruct((tok, 1), jnp.float32),
        ],
    )(*pieces, tokens, inv, norm_gain[None, :], cotangent, w_gate, w_up, w_down)


def hid_sum(value):
    size = lax.axis_size("hid")
    total = value
    for shift in range(1, size):
        pairs = [(source, (source + shift) % size) for source in range(size)]
        total = total + lax.ppermute(value, "hid", pairs)
    return total


def body(tokens, cotangent, blocks, coef_self, coef_cross, norm_gain, w_gate, w_up, w_down):
    tok, width = tokens.shape
    sections = lax.axis_size("seq").bit_length() - 1
    nblk = blocks.shape[0]
    blen = blocks.shape[1]
    tok_blocks = tokens.reshape(nblk, blen, width)
    chunks = CHUNKS if tok % CHUNKS == 0 else 1
    rows = tok // chunks
    spans = [slice(chunk * rows, (chunk + 1) * rows) for chunk in range(chunks)]
    states = [[None] * sections for _ in spans]
    mates = [[None] * sections for _ in spans]
    if nblk == 1:
        pieces = [
            jnp.einsum(
                "kij,kjd->kid", blocks[:, rs], tok_blocks, preferred_element_type=jnp.float32
            ).astype(jnp.bfloat16).reshape(rows, width)
            for rs in spans
        ]
    else:
        local = jnp.einsum(
            "kij,kjd->kid", blocks, tok_blocks, preferred_element_type=jnp.float32
        ).astype(jnp.bfloat16).reshape(tok, width)
        pieces = [local[rs] for rs in spans]
    for section in range(sections):
        for chunk, rs in enumerate(spans):
            value = pieces[chunk]
            mate = from_partner(value, "seq", section)
            states[chunk][section] = value
            mates[chunk][section] = mate
            pieces[chunk] = (
                coef_self[section, rs][:, None] * value.astype(jnp.float32)
                + coef_cross[section, rs][:, None] * mate.astype(jnp.float32)
            ).astype(jnp.bfloat16)
    current = jnp.concatenate(pieces, axis=0)
    tok_f = tokens.astype(jnp.float32)
    mixed_f = current.astype(jnp.float32)
    resid = tok_f + tok_f * mixed_f
    square = hid_sum(jnp.sum(resid * resid, axis=-1, keepdims=True))
    inv = lax.rsqrt(square / D + 1e-06)
    scaled, inner = ffn_grad(pieces, tokens, inv, norm_gain, cotangent, w_gate, w_up, w_down)
    inner = hid_sum(inner)
    d_resid = (
        cotangent.astype(jnp.float32)
        + inv * scaled
        - resid * (inv**3 * inner / D)
    )
    d_mixed = (d_resid * tok_f).astype(jnp.bfloat16)
    grads_self = [[None] * sections for _ in spans]
    grads_cross = [[None] * sections for _ in spans]
    backs = [d_mixed[rs] for rs in spans]
    for section in range(sections - 1, -1, -1):
        for chunk, rs in enumerate(spans):
            back_f = backs[chunk].astype(jnp.float32)
            grads_self[chunk][section] = jnp.sum(
                back_f * states[chunk][section].astype(jnp.float32), axis=-1
            )
            grads_cross[chunk][section] = jnp.sum(
                back_f * mates[chunk][section].astype(jnp.float32), axis=-1
            )
            sent = (coef_cross[section, rs][:, None] * back_f).astype(jnp.bfloat16)
            received = from_partner(sent, "seq", section)
            backs[chunk] = (
                coef_self[section, rs][:, None] * back_f + received.astype(jnp.float32)
            ).astype(jnp.bfloat16)
    back = jnp.concatenate(backs, axis=0)
    part_self = jnp.concatenate([jnp.stack(g) for g in grads_self], axis=1)
    part_cross = jnp.concatenate([jnp.stack(g) for g in grads_cross], axis=1)
    back_blocks = back.reshape(nblk, blen, width)
    part_blocks = jnp.einsum(
        "kid,kjd->kij", back_blocks, tok_blocks, preferred_element_type=jnp.float32
    )
    from_blocks = jnp.einsum(
        "kij,kid->kjd", blocks, back_blocks, preferred_element_type=jnp.float32
    ).reshape(tok, width)
    grad_self, grad_cross, grad_blocks = jax.tree.map(hid_sum, (part_self, part_cross, part_blocks))
    grad_x = (d_resid * (1.0 + mixed_f) + from_blocks).astype(jnp.bfloat16)
    return (grad_x, grad_self, grad_cross, grad_blocks)


def solution(mesh):
    return jax.shard_map(
        body,
        mesh=mesh,
        in_specs=(
            P(("groups", "seq"), "hid"),
            P(("groups", "seq"), "hid"),
            P("seq", None, None),
            P(None, "seq"),
            P(None, "seq"),
            P("hid"),
            P("hid", None, None),
            P("hid", None, None),
            P("hid", None, None),
        ),
        out_specs=(
            P(("groups", "seq"), "hid"),
            P(None, ("groups", "seq")),
            P(None, ("groups", "seq")),
            P(("groups", "seq"), None, None),
        ),
        check_vma=False,
    )
```

```python
import jax
import jax.numpy as jnp
from jax import lax
from jax.sharding import PartitionSpec as P
from jax.experimental import pallas as pl

D = 2048
CHUNKS = 2


def from_partner(value, axis, distance):
    mask = 2**distance
    pairs = [(source, source ^ mask) for source in range(lax.axis_size(axis))]
    return lax.ppermute(value, axis, pairs)


def ffn_kernel(normed_ref, cot_ref, wg_ref, wu_ref, wd_ref, out_ref):
    cblock = wg_ref.shape[1]
    contract_last = (((1,), (1,)), ((), ()))
    for group in range(wg_ref.shape[0]):
        cols = slice(group * cblock, (group + 1) * cblock)
        normed = normed_ref[:, cols]
        w_gate = wg_ref[group]
        w_up = wu_ref[group]
        gate_pre = jnp.dot(normed, w_gate, preferred_element_type=jnp.float32)
        up_val = jnp.dot(normed, w_up, preferred_element_type=jnp.float32)
        d_hidden = lax.dot_general(
            cot_ref[:, cols], wd_ref[group], contract_last, preferred_element_type=jnp.float32
        )
        sig = 1.0 / (1.0 + jnp.exp(-gate_pre))
        d_up = (d_hidden * gate_pre * sig).astype(jnp.bfloat16)
        d_gate = (d_hidden * up_val * sig * (1.0 + gate_pre * (1.0 - sig))).astype(jnp.bfloat16)
        out_ref[:, cols] = lax.dot_general(
            d_gate, w_gate, contract_last, preferred_element_type=jnp.float32
        ) + lax.dot_general(d_up, w_up, contract_last, preferred_element_type=jnp.float32)


def ffn_grad(normed, cotangent, w_gate, w_up, w_down, per_step=4):
    tok, width = normed.shape
    groups_here, cblock, hidden = w_gate.shape
    if groups_here % per_step:
        per_step = 1
    act = pl.BlockSpec((tok, cblock * per_step), lambda g: (0, g))
    return pl.pallas_call(
        ffn_kernel,
        grid=(groups_here // per_step,),
        in_specs=[
            act,
            act,
            pl.BlockSpec((per_step, cblock, hidden), lambda g: (g, 0, 0)),
            pl.BlockSpec((per_step, cblock, hidden), lambda g: (g, 0, 0)),
            pl.BlockSpec((per_step, hidden, cblock), lambda g: (g, 0, 0)),
        ],
        out_specs=act,
        out_shape=jax.ShapeDtypeStruct((tok, width), jnp.float32),
        cost_estimate=pl.CostEstimate(
            flops=10 * tok * cblock * hidden * groups_here,
            transcendentals=tok * hidden * groups_here,
            bytes_accessed=3 * groups_here * cblock * hidden * 2 + tok * width * 8,
        ),
    )(normed, cotangent, w_gate, w_up, w_down)


def hid_sum(value):
    size = lax.axis_size("hid")
    total = value
    for shift in range(1, size):
        pairs = [(source, (source + shift) % size) for source in range(size)]
        total = total + lax.ppermute(value, "hid", pairs)
    return total


def tie(value, after):
    if after is None:
        return value
    return lax.optimization_barrier((value, after))[0]


def body(tokens, cotangent, blocks, coef_self, coef_cross, norm_gain, w_gate, w_up, w_down):
    tok, width = tokens.shape
    sections = lax.axis_size("seq").bit_length() - 1
    nblk = blocks.shape[0]
    blen = blocks.shape[1]
    tok_blocks = tokens.reshape(nblk, blen, width)
    chunks = CHUNKS if tok % CHUNKS == 0 else 1
    rows = tok // chunks
    spans = [slice(chunk * rows, (chunk + 1) * rows) for chunk in range(chunks)]
    states = [[None] * sections for _ in spans]
    mates = [[None] * sections for _ in spans]
    if nblk == 1:
        pieces = [
            jnp.einsum(
                "kij,kjd->kid", blocks[:, rs], tok_blocks, preferred_element_type=jnp.float32
            ).astype(jnp.bfloat16).reshape(rows, width)
            for rs in spans
        ]
    else:
        local = jnp.einsum(
            "kij,kjd->kid", blocks, tok_blocks, preferred_element_type=jnp.float32
        ).astype(jnp.bfloat16).reshape(tok, width)
        pieces = [local[rs] for rs in spans]
    for section in range(sections):
        for chunk, rs in enumerate(spans):
            value = pieces[chunk]
            mate = from_partner(value, "seq", section)
            states[chunk][section] = value
            mates[chunk][section] = mate
            pieces[chunk] = (
                coef_self[section, rs][:, None] * value.astype(jnp.float32)
                + coef_cross[section, rs][:, None] * mate.astype(jnp.float32)
            ).astype(jnp.bfloat16)
    top = sections - 1
    backs = []
    sents = []
    directs = []
    previous = None
    for chunk, rs in enumerate(spans):
        mixed = tie(pieces[chunk], previous)
        cot = cotangent[rs]
        tok_f = tokens[rs].astype(jnp.float32)
        mixed_f = mixed.astype(jnp.float32)
        resid = tok_f + tok_f * mixed_f
        square = hid_sum(jnp.sum(resid * resid, axis=-1))
        inv = lax.rsqrt(square / D + 1e-06)
        normed = (resid * inv[:, None] * norm_gain).astype(jnp.bfloat16)
        d_normed = ffn_grad(normed, cot, w_gate, w_up, w_down)
        scaled = norm_gain * d_normed
        inner = hid_sum(jnp.sum(resid * scaled, axis=-1))
        d_resid = (
            cot.astype(jnp.float32)
            + inv[:, None] * scaled
            - resid * (inv**3 * inner / D)[:, None]
        )
        d_mixed = (d_resid * tok_f).astype(jnp.bfloat16)
        sent = (coef_cross[top, rs][:, None] * d_mixed.astype(jnp.float32)).astype(jnp.bfloat16)
        previous = sent
        backs.append(d_mixed)
        sents.append(sent)
        directs.append(d_resid * (1.0 + mixed_f))
    grads_self = [[None] * sections for _ in spans]
    grads_cross = [[None] * sections for _ in spans]
    for section in range(sections - 1, -1, -1):
        for chunk, rs in enumerate(spans):
            back_f = backs[chunk].astype(jnp.float32)
            grads_self[chunk][section] = jnp.sum(
                back_f * states[chunk][section].astype(jnp.float32), axis=-1
            )
            grads_cross[chunk][section] = jnp.sum(
                back_f * mates[chunk][section].astype(jnp.float32), axis=-1
            )
            if section == top:
                sent = sents[chunk]
            else:
                sent = (coef_cross[section, rs][:, None] * back_f).astype(jnp.bfloat16)
            received = from_partner(sent, "seq", section)
            backs[chunk] = (
                coef_self[section, rs][:, None] * back_f + received.astype(jnp.float32)
            ).astype(jnp.bfloat16)
    back = jnp.concatenate(backs, axis=0)
    part_self = jnp.concatenate([jnp.stack(g) for g in grads_self], axis=1)
    part_cross = jnp.concatenate([jnp.stack(g) for g in grads_cross], axis=1)
    back_blocks = back.reshape(nblk, blen, width)
    part_blocks = jnp.einsum(
        "kid,kjd->kij", back_blocks, tok_blocks, preferred_element_type=jnp.float32
    )
    from_blocks = jnp.einsum(
        "kij,kid->kjd", blocks, back_blocks, preferred_element_type=jnp.float32
    ).reshape(tok, width)
    grad_self, grad_cross, grad_blocks = jax.tree.map(hid_sum, (part_self, part_cross, part_blocks))
    grad_x = (jnp.concatenate(directs, axis=0) + from_blocks).astype(jnp.bfloat16)
    return (grad_x, grad_self, grad_cross, grad_blocks)


def solution(mesh):
    return jax.shard_map(
        body,
        mesh=mesh,
        in_specs=(
            P(("groups", "seq"), "hid"),
            P(("groups", "seq"), "hid"),
            P("seq", None, None),
            P(None, "seq"),
            P(None, "seq"),
            P("hid"),
            P("hid", None, None),
            P("hid", None, None),
            P("hid", None, None),
        ),
        out_specs=(
            P(("groups", "seq"), "hid"),
            P(None, ("groups", "seq")),
            P(None, ("groups", "seq")),
            P(("groups", "seq"), None, None),
        ),
        check_vma=False,
    )
```

```python
import jax
import jax.numpy as jnp
from jax import lax
from jax.sharding import PartitionSpec as P
from jax.experimental import pallas as pl

D = 2048
CHUNKS = 2


def from_partner(value, axis, distance):
    mask = 2**distance
    pairs = [(source, source ^ mask) for source in range(lax.axis_size(axis))]
    return lax.ppermute(value, axis, pairs)


def ffn_kernel(normed_ref, cot_ref, wg_ref, wu_ref, wd_ref, out_ref):
    cblock = wg_ref.shape[1]
    contract_last = (((1,), (1,)), ((), ()))
    for group in range(wg_ref.shape[0]):
        cols = slice(group * cblock, (group + 1) * cblock)
        normed = normed_ref[:, cols]
        w_gate = wg_ref[group]
        w_up = wu_ref[group]
        gate_pre = jnp.dot(normed, w_gate, preferred_element_type=jnp.float32)
        up_val = jnp.dot(normed, w_up, preferred_element_type=jnp.float32)
        d_hidden = lax.dot_general(
            cot_ref[:, cols], wd_ref[group], contract_last, preferred_element_type=jnp.float32
        )
        sig = 1.0 / (1.0 + jnp.exp(-gate_pre))
        d_up = (d_hidden * gate_pre * sig).astype(jnp.bfloat16)
        d_gate = (d_hidden * up_val * sig * (1.0 + gate_pre * (1.0 - sig))).astype(jnp.bfloat16)
        out_ref[:, cols] = lax.dot_general(
            d_gate, w_gate, contract_last, preferred_element_type=jnp.float32
        ) + lax.dot_general(d_up, w_up, contract_last, preferred_element_type=jnp.float32)


def ffn_grad(normed, cotangent, w_gate, w_up, w_down, per_step=4):
    tok, width = normed.shape
    groups_here, cblock, hidden = w_gate.shape
    if groups_here % per_step:
        per_step = 1
    act = pl.BlockSpec((tok, cblock * per_step), lambda g: (0, g))
    return pl.pallas_call(
        ffn_kernel,
        grid=(groups_here // per_step,),
        in_specs=[
            act,
            act,
            pl.BlockSpec((per_step, cblock, hidden), lambda g: (g, 0, 0)),
            pl.BlockSpec((per_step, cblock, hidden), lambda g: (g, 0, 0)),
            pl.BlockSpec((per_step, hidden, cblock), lambda g: (g, 0, 0)),
        ],
        out_specs=act,
        out_shape=jax.ShapeDtypeStruct((tok, width), jnp.float32),
        cost_estimate=pl.CostEstimate(
            flops=10 * tok * cblock * hidden * groups_here,
            transcendentals=tok * hidden * groups_here,
            bytes_accessed=3 * groups_here * cblock * hidden * 2 + tok * width * 8,
        ),
    )(normed, cotangent, w_gate, w_up, w_down)


def hid_sum(value):
    size = lax.axis_size("hid")
    total = value
    for shift in range(1, size):
        pairs = [(source, (source + shift) % size) for source in range(size)]
        total = total + lax.ppermute(value, "hid", pairs)
    return total


def tie(value, after):
    if after is None:
        return value
    return lax.optimization_barrier((value, after))[0]


def body(tokens, cotangent, blocks, coef_self, coef_cross, norm_gain, w_gate, w_up, w_down):
    tok, width = tokens.shape
    sections = lax.axis_size("seq").bit_length() - 1
    nblk = blocks.shape[0]
    blen = blocks.shape[1]
    tok_blocks = tokens.reshape(nblk, blen, width)
    chunks = CHUNKS if tok % CHUNKS == 0 else 1
    rows = tok // chunks
    spans = [slice(chunk * rows, (chunk + 1) * rows) for chunk in range(chunks)]
    states = [[None] * sections for _ in spans]
    mates = [[None] * sections for _ in spans]
    if nblk == 1:
        pieces = [
            jnp.einsum(
                "kij,kjd->kid", blocks[:, rs], tok_blocks, preferred_element_type=jnp.float32
            ).astype(jnp.bfloat16).reshape(rows, width)
            for rs in spans
        ]
    else:
        local = jnp.einsum(
            "kij,kjd->kid", blocks, tok_blocks, preferred_element_type=jnp.float32
        ).astype(jnp.bfloat16).reshape(tok, width)
        pieces = [local[rs] for rs in spans]
    for section in range(sections):
        for chunk, rs in enumerate(spans):
            value = pieces[chunk]
            mate = from_partner(value, "seq", section)
            states[chunk][section] = value
            mates[chunk][section] = mate
            pieces[chunk] = (
                coef_self[section, rs][:, None] * value.astype(jnp.float32)
                + coef_cross[section, rs][:, None] * mate.astype(jnp.float32)
            ).astype(jnp.bfloat16)
    top = sections - 1
    backs = []
    sents = []
    directs = []
    previous = None
    for chunk, rs in enumerate(spans):
        mixed = tie(pieces[chunk], previous)
        cot = cotangent[rs]
        tok_f = tokens[rs].astype(jnp.float32)
        mixed_f = mixed.astype(jnp.float32)
        resid = tok_f + tok_f * mixed_f
        reduce_hid = hid_sum if chunk == 0 else (lambda v: lax.psum(v, "hid"))
        square = reduce_hid(jnp.sum(resid * resid, axis=-1))
        inv = lax.rsqrt(square / D + 1e-06)
        normed = (resid * inv[:, None] * norm_gain).astype(jnp.bfloat16)
        d_normed = ffn_grad(normed, cot, w_gate, w_up, w_down)
        scaled = norm_gain * d_normed
        inner = reduce_hid(jnp.sum(resid * scaled, axis=-1))
        d_resid = (
            cot.astype(jnp.float32)
            + inv[:, None] * scaled
            - resid * (inv**3 * inner / D)[:, None]
        )
        d_mixed = (d_resid * tok_f).astype(jnp.bfloat16)
        sent = (coef_cross[top, rs][:, None] * d_mixed.astype(jnp.float32)).astype(jnp.bfloat16)
        previous = sent
        backs.append(d_mixed)
        sents.append(from_partner(sent, "seq", top))
        directs.append(d_resid * (1.0 + mixed_f))
    grads_self = [[None] * sections for _ in spans]
    grads_cross = [[None] * sections for _ in spans]
    for section in range(sections - 1, -1, -1):
        for chunk, rs in enumerate(spans):
            back_f = backs[chunk].astype(jnp.float32)
            grads_self[chunk][section] = jnp.sum(
                back_f * states[chunk][section].astype(jnp.float32), axis=-1
            )
            grads_cross[chunk][section] = jnp.sum(
                back_f * mates[chunk][section].astype(jnp.float32), axis=-1
            )
            if section == top:
                received = sents[chunk]
            else:
                sent = (coef_cross[section, rs][:, None] * back_f).astype(jnp.bfloat16)
                received = from_partner(sent, "seq", section)
            backs[chunk] = (
                coef_self[section, rs][:, None] * back_f + received.astype(jnp.float32)
            ).astype(jnp.bfloat16)
    back = jnp.concatenate(backs, axis=0)
    part_self = jnp.concatenate([jnp.stack(g) for g in grads_self], axis=1)
    part_cross = jnp.concatenate([jnp.stack(g) for g in grads_cross], axis=1)
    back_blocks = back.reshape(nblk, blen, width)
    part_blocks = jnp.einsum(
        "kid,kjd->kij", back_blocks, tok_blocks, preferred_element_type=jnp.float32
    )
    from_blocks = jnp.einsum(
        "kij,kid->kjd", blocks, back_blocks, preferred_element_type=jnp.float32
    ).reshape(tok, width)
    grad_self, grad_cross, grad_blocks = jax.tree.map(hid_sum, (part_self, part_cross, part_blocks))
    grad_x = (jnp.concatenate(directs, axis=0) + from_blocks).astype(jnp.bfloat16)
    return (grad_x, grad_self, grad_cross, grad_blocks)


def solution(mesh):
    return jax.shard_map(
        body,
        mesh=mesh,
        in_specs=(
            P(("groups", "seq"), "hid"),
            P(("groups", "seq"), "hid"),
            P("seq", None, None),
            P(None, "seq"),
            P(None, "seq"),
            P("hid"),
            P("hid", None, None),
            P("hid", None, None),
            P("hid", None, None),
        ),
        out_specs=(
            P(("groups", "seq"), "hid"),
            P(None, ("groups", "seq")),
            P(None, ("groups", "seq")),
            P(("groups", "seq"), None, None),
        ),
        check_vma=False,
    )
```

```python
import jax
import jax.numpy as jnp
from jax import lax
from jax.sharding import PartitionSpec as P
from jax.experimental import pallas as pl

D = 2048
CHUNKS = 2


def from_partner(value, axis, distance):
    mask = 2**distance
    pairs = [(source, source ^ mask) for source in range(lax.axis_size(axis))]
    return lax.ppermute(value, axis, pairs)


def ffn_kernel(normed_ref, cot_ref, wg_ref, wu_ref, wd_ref, out_ref):
    cblock = wg_ref.shape[1]
    contract_last = (((1,), (1,)), ((), ()))
    for group in range(wg_ref.shape[0]):
        cols = slice(group * cblock, (group + 1) * cblock)
        normed = normed_ref[:, cols]
        w_gate = wg_ref[group]
        w_up = wu_ref[group]
        gate_pre = jnp.dot(normed, w_gate, preferred_element_type=jnp.float32)
        up_val = jnp.dot(normed, w_up, preferred_element_type=jnp.float32)
        d_hidden = lax.dot_general(
            cot_ref[:, cols], wd_ref[group], contract_last, preferred_element_type=jnp.float32
        )
        sig = 1.0 / (1.0 + jnp.exp(-gate_pre))
        d_up = (d_hidden * gate_pre * sig).astype(jnp.bfloat16)
        d_gate = (d_hidden * up_val * sig * (1.0 + gate_pre * (1.0 - sig))).astype(jnp.bfloat16)
        out_ref[:, cols] = lax.dot_general(
            d_gate, w_gate, contract_last, preferred_element_type=jnp.float32
        ) + lax.dot_general(d_up, w_up, contract_last, preferred_element_type=jnp.float32)


def ffn_grad(normed, cotangent, w_gate, w_up, w_down, per_step=4):
    tok, width = normed.shape
    groups_here, cblock, hidden = w_gate.shape
    if groups_here % per_step:
        per_step = 1
    act = pl.BlockSpec((tok, cblock * per_step), lambda g: (0, g))
    return pl.pallas_call(
        ffn_kernel,
        grid=(groups_here // per_step,),
        in_specs=[
            act,
            act,
            pl.BlockSpec((per_step, cblock, hidden), lambda g: (g, 0, 0)),
            pl.BlockSpec((per_step, cblock, hidden), lambda g: (g, 0, 0)),
            pl.BlockSpec((per_step, hidden, cblock), lambda g: (g, 0, 0)),
        ],
        out_specs=act,
        out_shape=jax.ShapeDtypeStruct((tok, width), jnp.float32),
        cost_estimate=pl.CostEstimate(
            flops=10 * tok * cblock * hidden * groups_here,
            transcendentals=tok * hidden * groups_here,
            bytes_accessed=3 * groups_here * cblock * hidden * 2 + tok * width * 8,
        ),
    )(normed, cotangent, w_gate, w_up, w_down)


def hid_sum(value):
    size = lax.axis_size("hid")
    total = value
    for shift in range(1, size):
        pairs = [(source, (source + shift) % size) for source in range(size)]
        total = total + lax.ppermute(value, "hid", pairs)
    return total


def tie(value, after):
    if after is None:
        return value
    return lax.optimization_barrier((value, after))[0]


def body(tokens, cotangent, blocks, coef_self, coef_cross, norm_gain, w_gate, w_up, w_down):
    tok, width = tokens.shape
    sections = lax.axis_size("seq").bit_length() - 1
    nblk = blocks.shape[0]
    blen = blocks.shape[1]
    tok_blocks = tokens.reshape(nblk, blen, width)
    chunks = CHUNKS if tok % CHUNKS == 0 else 1
    rows = tok // chunks
    spans = [slice(chunk * rows, (chunk + 1) * rows) for chunk in range(chunks)]
    states = [[None] * sections for _ in spans]
    mates = [[None] * sections for _ in spans]
    if nblk == 1:
        pieces = [
            jnp.einsum(
                "kij,kjd->kid", blocks[:, rs], tok_blocks, preferred_element_type=jnp.float32
            ).astype(jnp.bfloat16).reshape(rows, width)
            for rs in spans
        ]
    else:
        local = jnp.einsum(
            "kij,kjd->kid", blocks, tok_blocks, preferred_element_type=jnp.float32
        ).astype(jnp.bfloat16).reshape(tok, width)
        pieces = [local[rs] for rs in spans]
    for section in range(sections):
        for chunk, rs in enumerate(spans):
            value = pieces[chunk]
            mate = from_partner(value, "seq", section)
            states[chunk][section] = value
            mates[chunk][section] = mate
            pieces[chunk] = (
                coef_self[section, rs][:, None] * value.astype(jnp.float32)
                + coef_cross[section, rs][:, None] * mate.astype(jnp.float32)
            ).astype(jnp.bfloat16)
    top = sections - 1
    backs = []
    sents = []
    directs = []
    previous = None
    for chunk, rs in enumerate(spans):
        mixed = tie(pieces[chunk], previous)
        cot = cotangent[rs]
        tok_f = tokens[rs].astype(jnp.float32)
        mixed_f = mixed.astype(jnp.float32)
        resid = tok_f + tok_f * mixed_f
        reduce_hid = hid_sum if chunk == 0 else (lambda v: lax.psum(v, "hid"))
        square = hid_sum(jnp.sum(resid * resid, axis=-1))
        inv = lax.rsqrt(square / D + 1e-06)
        normed = (resid * inv[:, None] * norm_gain).astype(jnp.bfloat16)
        d_normed = ffn_grad(normed, cot, w_gate, w_up, w_down)
        scaled = norm_gain * d_normed
        inner = reduce_hid(jnp.sum(resid * scaled, axis=-1))
        d_resid = (
            cot.astype(jnp.float32)
            + inv[:, None] * scaled
            - resid * (inv**3 * inner / D)[:, None]
        )
        d_mixed = (d_resid * tok_f).astype(jnp.bfloat16)
        sent = (coef_cross[top, rs][:, None] * d_mixed.astype(jnp.float32)).astype(jnp.bfloat16)
        previous = sent
        backs.append(d_mixed)
        sents.append(from_partner(sent, "seq", top))
        directs.append(d_resid * (1.0 + mixed_f))
    grads_self = [[None] * sections for _ in spans]
    grads_cross = [[None] * sections for _ in spans]
    for section in range(sections - 1, -1, -1):
        for chunk, rs in enumerate(spans):
            back_f = backs[chunk].astype(jnp.float32)
            grads_self[chunk][section] = jnp.sum(
                back_f * states[chunk][section].astype(jnp.float32), axis=-1
            )
            grads_cross[chunk][section] = jnp.sum(
                back_f * mates[chunk][section].astype(jnp.float32), axis=-1
            )
            if section == top:
                received = sents[chunk]
            else:
                sent = (coef_cross[section, rs][:, None] * back_f).astype(jnp.bfloat16)
                received = from_partner(sent, "seq", section)
            backs[chunk] = (
                coef_self[section, rs][:, None] * back_f + received.astype(jnp.float32)
            ).astype(jnp.bfloat16)
    back = jnp.concatenate(backs, axis=0)
    part_self = jnp.concatenate([jnp.stack(g) for g in grads_self], axis=1)
    part_cross = jnp.concatenate([jnp.stack(g) for g in grads_cross], axis=1)
    back_blocks = back.reshape(nblk, blen, width)
    part_blocks = jnp.einsum(
        "kid,kjd->kij", back_blocks, tok_blocks, preferred_element_type=jnp.float32
    )
    from_blocks = jnp.einsum(
        "kij,kid->kjd", blocks, back_blocks, preferred_element_type=jnp.float32
    ).reshape(tok, width)
    grad_self, grad_cross, grad_blocks = jax.tree.map(hid_sum, (part_self, part_cross, part_blocks))
    grad_x = (jnp.concatenate(directs, axis=0) + from_blocks).astype(jnp.bfloat16)
    return (grad_x, grad_self, grad_cross, grad_blocks)


def solution(mesh):
    return jax.shard_map(
        body,
        mesh=mesh,
        in_specs=(
            P(("groups", "seq"), "hid"),
            P(("groups", "seq"), "hid"),
            P("seq", None, None),
            P(None, "seq"),
            P(None, "seq"),
            P("hid"),
            P("hid", None, None),
            P("hid", None, None),
            P("hid", None, None),
        ),
        out_specs=(
            P(("groups", "seq"), "hid"),
            P(None, ("groups", "seq")),
            P(None, ("groups", "seq")),
            P(("groups", "seq"), None, None),
        ),
        check_vma=False,
    )
```

```python
import jax
import jax.numpy as jnp
from jax import lax
from jax.sharding import PartitionSpec as P
from jax.experimental import pallas as pl

D = 2048
CHUNKS = 2


def from_partner(value, axis, distance):
    mask = 2**distance
    pairs = [(source, source ^ mask) for source in range(lax.axis_size(axis))]
    return lax.ppermute(value, axis, pairs)


def ffn_kernel(normed_ref, cot_ref, wg_ref, wu_ref, wd_ref, out_ref):
    cblock = wg_ref.shape[1]
    contract_last = (((1,), (1,)), ((), ()))
    for group in range(wg_ref.shape[0]):
        cols = slice(group * cblock, (group + 1) * cblock)
        normed = normed_ref[:, cols]
        w_gate = wg_ref[group]
        w_up = wu_ref[group]
        gate_pre = jnp.dot(normed, w_gate, preferred_element_type=jnp.float32)
        up_val = jnp.dot(normed, w_up, preferred_element_type=jnp.float32)
        d_hidden = lax.dot_general(
            cot_ref[:, cols], wd_ref[group], contract_last, preferred_element_type=jnp.float32
        )
        sig = 1.0 / (1.0 + jnp.exp(-gate_pre))
        d_up = (d_hidden * gate_pre * sig).astype(jnp.bfloat16)
        d_gate = (d_hidden * up_val * sig * (1.0 + gate_pre * (1.0 - sig))).astype(jnp.bfloat16)
        out_ref[:, cols] = lax.dot_general(
            d_gate, w_gate, contract_last, preferred_element_type=jnp.float32
        ) + lax.dot_general(d_up, w_up, contract_last, preferred_element_type=jnp.float32)


def ffn_grad(normed, cotangent, w_gate, w_up, w_down, per_step=4):
    tok, width = normed.shape
    groups_here, cblock, hidden = w_gate.shape
    if groups_here % per_step:
        per_step = 1
    act = pl.BlockSpec((tok, cblock * per_step), lambda g: (0, g))
    return pl.pallas_call(
        ffn_kernel,
        grid=(groups_here // per_step,),
        in_specs=[
            act,
            act,
            pl.BlockSpec((per_step, cblock, hidden), lambda g: (g, 0, 0)),
            pl.BlockSpec((per_step, cblock, hidden), lambda g: (g, 0, 0)),
            pl.BlockSpec((per_step, hidden, cblock), lambda g: (g, 0, 0)),
        ],
        out_specs=act,
        out_shape=jax.ShapeDtypeStruct((tok, width), jnp.float32),
        cost_estimate=pl.CostEstimate(
            flops=10 * tok * cblock * hidden * groups_here,
            transcendentals=tok * hidden * groups_here,
            bytes_accessed=3 * groups_here * cblock * hidden * 2 + tok * width * 8,
        ),
    )(normed, cotangent, w_gate, w_up, w_down)


def hid_sum(value):
    size = lax.axis_size("hid")
    total = value
    for shift in range(1, size):
        pairs = [(source, (source + shift) % size) for source in range(size)]
        total = total + lax.ppermute(value, "hid", pairs)
    return total


def tie(value, after):
    if after is None:
        return value
    return lax.optimization_barrier((value, after))[0]


def body(tokens, cotangent, blocks, coef_self, coef_cross, norm_gain, w_gate, w_up, w_down):
    tok, width = tokens.shape
    sections = lax.axis_size("seq").bit_length() - 1
    nblk = blocks.shape[0]
    blen = blocks.shape[1]
    tok_blocks = tokens.reshape(nblk, blen, width)
    first = (tok * 5 // 8) // 16 * 16
    if CHUNKS == 2 and 0 < first < tok:
        spans = [slice(0, first), slice(first, tok)]
    else:
        spans = [slice(0, tok)]
    states = [[None] * sections for _ in spans]
    mates = [[None] * sections for _ in spans]
    if nblk == 1:
        pieces = [
            jnp.einsum(
                "kij,kjd->kid", blocks[:, rs], tok_blocks, preferred_element_type=jnp.float32
            ).astype(jnp.bfloat16).reshape(rs.stop - rs.start, width)
            for rs in spans
        ]
    else:
        local = jnp.einsum(
            "kij,kjd->kid", blocks, tok_blocks, preferred_element_type=jnp.float32
        ).astype(jnp.bfloat16).reshape(tok, width)
        pieces = [local[rs] for rs in spans]
    for section in range(sections):
        for chunk, rs in enumerate(spans):
            value = pieces[chunk]
            mate = from_partner(value, "seq", section)
            states[chunk][section] = value
            mates[chunk][section] = mate
            pieces[chunk] = (
                coef_self[section, rs][:, None] * value.astype(jnp.float32)
                + coef_cross[section, rs][:, None] * mate.astype(jnp.float32)
            ).astype(jnp.bfloat16)
    top = sections - 1
    backs = []
    sents = []
    directs = []
    previous = None
    for chunk, rs in enumerate(spans):
        mixed = tie(pieces[chunk], previous)
        cot = cotangent[rs]
        tok_f = tokens[rs].astype(jnp.float32)
        mixed_f = mixed.astype(jnp.float32)
        resid = tok_f + tok_f * mixed_f
        reduce_hid = hid_sum if chunk == 0 else (lambda v: lax.psum(v, "hid"))
        square = hid_sum(jnp.sum(resid * resid, axis=-1))
        inv = lax.rsqrt(square / D + 1e-06)
        normed = (resid * inv[:, None] * norm_gain).astype(jnp.bfloat16)
        d_normed = ffn_grad(normed, cot, w_gate, w_up, w_down)
        scaled = norm_gain * d_normed
        inner = reduce_hid(jnp.sum(resid * scaled, axis=-1))
        d_resid = (
            cot.astype(jnp.float32)
            + inv[:, None] * scaled
            - resid * (inv**3 * inner / D)[:, None]
        )
        d_mixed = (d_resid * tok_f).astype(jnp.bfloat16)
        sent = (coef_cross[top, rs][:, None] * d_mixed.astype(jnp.float32)).astype(jnp.bfloat16)
        previous = sent
        backs.append(d_mixed)
        sents.append(from_partner(sent, "seq", top))
        directs.append(d_resid * (1.0 + mixed_f))
    grads_self = [[None] * sections for _ in spans]
    grads_cross = [[None] * sections for _ in spans]
    for section in range(sections - 1, -1, -1):
        for chunk, rs in enumerate(spans):
            back_f = backs[chunk].astype(jnp.float32)
            grads_self[chunk][section] = jnp.sum(
                back_f * states[chunk][section].astype(jnp.float32), axis=-1
            )
            grads_cross[chunk][section] = jnp.sum(
                back_f * mates[chunk][section].astype(jnp.float32), axis=-1
            )
            if section == top:
                received = sents[chunk]
            else:
                sent = (coef_cross[section, rs][:, None] * back_f).astype(jnp.bfloat16)
                received = from_partner(sent, "seq", section)
            backs[chunk] = (
                coef_self[section, rs][:, None] * back_f + received.astype(jnp.float32)
            ).astype(jnp.bfloat16)
    back = jnp.concatenate(backs, axis=0)
    part_self = jnp.concatenate([jnp.stack(g) for g in grads_self], axis=1)
    part_cross = jnp.concatenate([jnp.stack(g) for g in grads_cross], axis=1)
    back_blocks = back.reshape(nblk, blen, width)
    part_blocks = jnp.einsum(
        "kid,kjd->kij", back_blocks, tok_blocks, preferred_element_type=jnp.float32
    )
    from_blocks = jnp.einsum(
        "kij,kid->kjd", blocks, back_blocks, preferred_element_type=jnp.float32
    ).reshape(tok, width)
    grad_self, grad_cross, grad_blocks = jax.tree.map(hid_sum, (part_self, part_cross, part_blocks))
    grad_x = (jnp.concatenate(directs, axis=0) + from_blocks).astype(jnp.bfloat16)
    return (grad_x, grad_self, grad_cross, grad_blocks)


def solution(mesh):
    return jax.shard_map(
        body,
        mesh=mesh,
        in_specs=(
            P(("groups", "seq"), "hid"),
            P(("groups", "seq"), "hid"),
            P("seq", None, None),
            P(None, "seq"),
            P(None, "seq"),
            P("hid"),
            P("hid", None, None),
            P("hid", None, None),
            P("hid", None, None),
        ),
        out_specs=(
            P(("groups", "seq"), "hid"),
            P(None, ("groups", "seq")),
            P(None, ("groups", "seq")),
            P(("groups", "seq"), None, None),
        ),
        check_vma=False,
    )
```

```python
import jax
import jax.numpy as jnp
from jax import lax
from jax.sharding import PartitionSpec as P
from jax.experimental import pallas as pl

D = 2048
CHUNKS = 2


def from_partner(value, axis, distance):
    mask = 2**distance
    pairs = [(source, source ^ mask) for source in range(lax.axis_size(axis))]
    return lax.ppermute(value, axis, pairs)


def ffn_kernel(normed_ref, cot_ref, wgu_ref, wd_ref, out_ref):
    cblock = wgu_ref.shape[1]
    hidden = wd_ref.shape[1]
    contract_last = (((1,), (1,)), ((), ()))
    for group in range(wgu_ref.shape[0]):
        cols = slice(group * cblock, (group + 1) * cblock)
        w_both = wgu_ref[group]
        both = jnp.dot(normed_ref[:, cols], w_both, preferred_element_type=jnp.float32)
        gate_pre = both[:, :hidden]
        up_val = both[:, hidden:]
        d_hidden = lax.dot_general(
            cot_ref[:, cols], wd_ref[group], contract_last, preferred_element_type=jnp.float32
        )
        sig = 1.0 / (1.0 + jnp.exp(-gate_pre))
        d_up = (d_hidden * gate_pre * sig).astype(jnp.bfloat16)
        d_gate = (d_hidden * up_val * sig * (1.0 + gate_pre * (1.0 - sig))).astype(jnp.bfloat16)
        d_both = jnp.concatenate([d_gate, d_up], axis=1)
        out_ref[:, cols] = lax.dot_general(
            d_both, w_both, contract_last, preferred_element_type=jnp.float32
        )


def ffn_grad(normed, cotangent, w_both, w_down, per_step=4):
    tok, width = normed.shape
    groups_here, cblock, hidden2 = w_both.shape
    hidden = w_down.shape[1]
    if groups_here % per_step:
        per_step = 1
    act = pl.BlockSpec((tok, cblock * per_step), lambda g: (0, g))
    return pl.pallas_call(
        ffn_kernel,
        grid=(groups_here // per_step,),
        in_specs=[
            act,
            act,
            pl.BlockSpec((per_step, cblock, hidden2), lambda g: (g, 0, 0)),
            pl.BlockSpec((per_step, hidden, cblock), lambda g: (g, 0, 0)),
        ],
        out_specs=act,
        out_shape=jax.ShapeDtypeStruct((tok, width), jnp.float32),
        cost_estimate=pl.CostEstimate(
            flops=10 * tok * cblock * hidden * groups_here,
            transcendentals=tok * hidden * groups_here,
            bytes_accessed=3 * groups_here * cblock * hidden * 2 + tok * width * 8,
        ),
    )(normed, cotangent, w_both, w_down)


def hid_sum(value):
    size = lax.axis_size("hid")
    total = value
    for shift in range(1, size):
        pairs = [(source, (source + shift) % size) for source in range(size)]
        total = total + lax.ppermute(value, "hid", pairs)
    return total


def tie(value, after):
    if after is None:
        return value
    return lax.optimization_barrier((value, after))[0]


def body(tokens, cotangent, blocks, coef_self, coef_cross, norm_gain, w_gate, w_up, w_down):
    tok, width = tokens.shape
    sections = lax.axis_size("seq").bit_length() - 1
    nblk = blocks.shape[0]
    blen = blocks.shape[1]
    tok_blocks = tokens.reshape(nblk, blen, width)
    w_both = jnp.concatenate([w_gate, w_up], axis=-1)
    chunks = CHUNKS if tok % CHUNKS == 0 else 1
    rows = tok // chunks
    spans = [slice(chunk * rows, (chunk + 1) * rows) for chunk in range(chunks)]
    states = [[None] * sections for _ in spans]
    mates = [[None] * sections for _ in spans]
    if nblk == 1:
        pieces = [
            jnp.einsum(
                "kij,kjd->kid", blocks[:, rs], tok_blocks, preferred_element_type=jnp.float32
            ).astype(jnp.bfloat16).reshape(rows, width)
            for rs in spans
        ]
    else:
        local = jnp.einsum(
            "kij,kjd->kid", blocks, tok_blocks, preferred_element_type=jnp.float32
        ).astype(jnp.bfloat16).reshape(tok, width)
        pieces = [local[rs] for rs in spans]
    for section in range(sections):
        for chunk, rs in enumerate(spans):
            value = pieces[chunk]
            mate = from_partner(value, "seq", section)
            states[chunk][section] = value
            mates[chunk][section] = mate
            pieces[chunk] = (
                coef_self[section, rs][:, None] * value.astype(jnp.float32)
                + coef_cross[section, rs][:, None] * mate.astype(jnp.float32)
            ).astype(jnp.bfloat16)
    top = sections - 1
    backs = []
    sents = []
    directs = []
    previous = None
    for chunk, rs in enumerate(spans):
        mixed = tie(pieces[chunk], previous)
        cot = cotangent[rs]
        tok_f = tokens[rs].astype(jnp.float32)
        mixed_f = mixed.astype(jnp.float32)
        resid = tok_f + tok_f * mixed_f
        reduce_hid = hid_sum if chunk == 0 else (lambda v: lax.psum(v, "hid"))
        square = hid_sum(jnp.sum(resid * resid, axis=-1))
        inv = lax.rsqrt(square / D + 1e-06)
        normed = (resid * inv[:, None] * norm_gain).astype(jnp.bfloat16)
        d_normed = ffn_grad(normed, cot, w_both, w_down)
        scaled = norm_gain * d_normed
        inner = reduce_hid(jnp.sum(resid * scaled, axis=-1))
        d_resid = (
            cot.astype(jnp.float32)
            + inv[:, None] * scaled
            - resid * (inv**3 * inner / D)[:, None]
        )
        d_mixed = (d_resid * tok_f).astype(jnp.bfloat16)
        sent = (coef_cross[top, rs][:, None] * d_mixed.astype(jnp.float32)).astype(jnp.bfloat16)
        previous = sent
        backs.append(d_mixed)
        sents.append(from_partner(sent, "seq", top))
        directs.append(d_resid * (1.0 + mixed_f))
    grads_self = [[None] * sections for _ in spans]
    grads_cross = [[None] * sections for _ in spans]
    for section in range(sections - 1, -1, -1):
        for chunk, rs in enumerate(spans):
            back_f = backs[chunk].astype(jnp.float32)
            grads_self[chunk][section] = jnp.sum(
                back_f * states[chunk][section].astype(jnp.float32), axis=-1
            )
            grads_cross[chunk][section] = jnp.sum(
                back_f * mates[chunk][section].astype(jnp.float32), axis=-1
            )
            if section == top:
                received = sents[chunk]
            else:
                sent = (coef_cross[section, rs][:, None] * back_f).astype(jnp.bfloat16)
                received = from_partner(sent, "seq", section)
            backs[chunk] = (
                coef_self[section, rs][:, None] * back_f + received.astype(jnp.float32)
            ).astype(jnp.bfloat16)
    back = jnp.concatenate(backs, axis=0)
    part_self = jnp.concatenate([jnp.stack(g) for g in grads_self], axis=1)
    part_cross = jnp.concatenate([jnp.stack(g) for g in grads_cross], axis=1)
    back_blocks = back.reshape(nblk, blen, width)
    part_blocks = jnp.einsum(
        "kid,kjd->kij", back_blocks, tok_blocks, preferred_element_type=jnp.float32
    )
    from_blocks = jnp.einsum(
        "kij,kid->kjd", blocks, back_blocks, preferred_element_type=jnp.float32
    ).reshape(tok, width)
    grad_self, grad_cross, grad_blocks = jax.tree.map(hid_sum, (part_self, part_cross, part_blocks))
    grad_x = (jnp.concatenate(directs, axis=0) + from_blocks).astype(jnp.bfloat16)
    return (grad_x, grad_self, grad_cross, grad_blocks)


def solution(mesh):
    return jax.shard_map(
        body,
        mesh=mesh,
        in_specs=(
            P(("groups", "seq"), "hid"),
            P(("groups", "seq"), "hid"),
            P("seq", None, None),
            P(None, "seq"),
            P(None, "seq"),
            P("hid"),
            P("hid", None, None),
            P("hid", None, None),
            P("hid", None, None),
        ),
        out_specs=(
            P(("groups", "seq"), "hid"),
            P(None, ("groups", "seq")),
            P(None, ("groups", "seq")),
            P(("groups", "seq"), None, None),
        ),
        check_vma=False,
    )
```

```python
import jax
import jax.numpy as jnp
from jax import lax
from jax.sharding import PartitionSpec as P
from jax.experimental import pallas as pl
from jax.experimental.pallas import tpu as pltpu

D = 2048
CHUNKS = 2


def from_partner(value, axis, distance):
    mask = 2**distance
    pairs = [(source, source ^ mask) for source in range(lax.axis_size(axis))]
    return lax.ppermute(value, axis, pairs)


def ffn_kernel(normed_ref, cot_ref, wg_ref, wu_ref, wd_ref, out_ref):
    cblock = wg_ref.shape[1]
    contract_last = (((1,), (1,)), ((), ()))
    for group in range(wg_ref.shape[0]):
        cols = slice(group * cblock, (group + 1) * cblock)
        normed = normed_ref[:, cols]
        w_gate = wg_ref[group]
        w_up = wu_ref[group]
        gate_pre = jnp.dot(normed, w_gate, preferred_element_type=jnp.float32)
        up_val = jnp.dot(normed, w_up, preferred_element_type=jnp.float32)
        d_hidden = lax.dot_general(
            cot_ref[:, cols], wd_ref[group], contract_last, preferred_element_type=jnp.float32
        )
        sig = 1.0 / (1.0 + jnp.exp(-gate_pre))
        d_up = (d_hidden * gate_pre * sig).astype(jnp.bfloat16)
        d_gate = (d_hidden * up_val * sig * (1.0 + gate_pre * (1.0 - sig))).astype(jnp.bfloat16)
        out_ref[:, cols] = lax.dot_general(
            d_gate, w_gate, contract_last, preferred_element_type=jnp.float32
        ) + lax.dot_general(d_up, w_up, contract_last, preferred_element_type=jnp.float32)


def ffn_grad(normed, cotangent, w_gate, w_up, w_down):
    tok, width = normed.shape
    groups_here, cblock, hidden = w_gate.shape
    whole = pl.BlockSpec(memory_space=pltpu.VMEM)
    return pl.pallas_call(
        ffn_kernel,
        in_specs=[whole] * 5,
        out_specs=whole,
        out_shape=jax.ShapeDtypeStruct((tok, width), jnp.float32),
        cost_estimate=pl.CostEstimate(
            flops=10 * tok * cblock * hidden * groups_here,
            transcendentals=tok * hidden * groups_here,
            bytes_accessed=3 * groups_here * cblock * hidden * 2 + tok * width * 8,
        ),
    )(normed, cotangent, w_gate, w_up, w_down)


def hid_sum(value):
    size = lax.axis_size("hid")
    total = value
    for shift in range(1, size):
        pairs = [(source, (source + shift) % size) for source in range(size)]
        total = total + lax.ppermute(value, "hid", pairs)
    return total


def tie(value, after):
    if after is None:
        return value
    return lax.optimization_barrier((value, after))[0]


def body(tokens, cotangent, blocks, coef_self, coef_cross, norm_gain, w_gate, w_up, w_down):
    tok, width = tokens.shape
    sections = lax.axis_size("seq").bit_length() - 1
    nblk = blocks.shape[0]
    blen = blocks.shape[1]
    tok_blocks = tokens.reshape(nblk, blen, width)
    chunks = CHUNKS if tok % CHUNKS == 0 else 1
    rows = tok // chunks
    spans = [slice(chunk * rows, (chunk + 1) * rows) for chunk in range(chunks)]
    states = [[None] * sections for _ in spans]
    mates = [[None] * sections for _ in spans]
    if nblk == 1:
        pieces = [
            jnp.einsum(
                "kij,kjd->kid", blocks[:, rs], tok_blocks, preferred_element_type=jnp.float32
            ).astype(jnp.bfloat16).reshape(rows, width)
            for rs in spans
        ]
    else:
        local = jnp.einsum(
            "kij,kjd->kid", blocks, tok_blocks, preferred_element_type=jnp.float32
        ).astype(jnp.bfloat16).reshape(tok, width)
        pieces = [local[rs] for rs in spans]
    for section in range(sections):
        for chunk, rs in enumerate(spans):
            value = pieces[chunk]
            mate = from_partner(value, "seq", section)
            states[chunk][section] = value
            mates[chunk][section] = mate
            pieces[chunk] = (
                coef_self[section, rs][:, None] * value.astype(jnp.float32)
                + coef_cross[section, rs][:, None] * mate.astype(jnp.float32)
            ).astype(jnp.bfloat16)
    top = sections - 1
    backs = []
    sents = []
    directs = []
    previous = None
    for chunk, rs in enumerate(spans):
        mixed = tie(pieces[chunk], previous)
        cot = cotangent[rs]
        tok_f = tokens[rs].astype(jnp.float32)
        mixed_f = mixed.astype(jnp.float32)
        resid = tok_f + tok_f * mixed_f
        reduce_hid = hid_sum if chunk == 0 else (lambda v: lax.psum(v, "hid"))
        square = hid_sum(jnp.sum(resid * resid, axis=-1))
        inv = lax.rsqrt(square / D + 1e-06)
        normed = (resid * inv[:, None] * norm_gain).astype(jnp.bfloat16)
        d_normed = ffn_grad(normed, cot, w_gate, w_up, w_down)
        scaled = norm_gain * d_normed
        inner = reduce_hid(jnp.sum(resid * scaled, axis=-1))
        d_resid = (
            cot.astype(jnp.float32)
            + inv[:, None] * scaled
            - resid * (inv**3 * inner / D)[:, None]
        )
        d_mixed = (d_resid * tok_f).astype(jnp.bfloat16)
        sent = (coef_cross[top, rs][:, None] * d_mixed.astype(jnp.float32)).astype(jnp.bfloat16)
        previous = sent
        backs.append(d_mixed)
        sents.append(from_partner(sent, "seq", top))
        directs.append(d_resid * (1.0 + mixed_f))
    grads_self = [[None] * sections for _ in spans]
    grads_cross = [[None] * sections for _ in spans]
    for section in range(sections - 1, -1, -1):
        for chunk, rs in enumerate(spans):
            back_f = backs[chunk].astype(jnp.float32)
            grads_self[chunk][section] = jnp.sum(
                back_f * states[chunk][section].astype(jnp.float32), axis=-1
            )
            grads_cross[chunk][section] = jnp.sum(
                back_f * mates[chunk][section].astype(jnp.float32), axis=-1
            )
            if section == top:
                received = sents[chunk]
            else:
                sent = (coef_cross[section, rs][:, None] * back_f).astype(jnp.bfloat16)
                received = from_partner(sent, "seq", section)
            backs[chunk] = (
                coef_self[section, rs][:, None] * back_f + received.astype(jnp.float32)
            ).astype(jnp.bfloat16)
    back = jnp.concatenate(backs, axis=0)
    part_self = jnp.concatenate([jnp.stack(g) for g in grads_self], axis=1)
    part_cross = jnp.concatenate([jnp.stack(g) for g in grads_cross], axis=1)
    back_blocks = back.reshape(nblk, blen, width)
    part_blocks = jnp.einsum(
        "kid,kjd->kij", back_blocks, tok_blocks, preferred_element_type=jnp.float32
    )
    from_blocks = jnp.einsum(
        "kij,kid->kjd", blocks, back_blocks, preferred_element_type=jnp.float32
    ).reshape(tok, width)
    grad_self, grad_cross, grad_blocks = jax.tree.map(hid_sum, (part_self, part_cross, part_blocks))
    grad_x = (jnp.concatenate(directs, axis=0) + from_blocks).astype(jnp.bfloat16)
    return (grad_x, grad_self, grad_cross, grad_blocks)


def solution(mesh):
    return jax.shard_map(
        body,
        mesh=mesh,
        in_specs=(
            P(("groups", "seq"), "hid"),
            P(("groups", "seq"), "hid"),
            P("seq", None, None),
            P(None, "seq"),
            P(None, "seq"),
            P("hid"),
            P("hid", None, None),
            P("hid", None, None),
            P("hid", None, None),
        ),
        out_specs=(
            P(("groups", "seq"), "hid"),
            P(None, ("groups", "seq")),
            P(None, ("groups", "seq")),
            P(("groups", "seq"), None, None),
        ),
        check_vma=False,
    )
```

```python
import jax
import jax.numpy as jnp
from jax import lax
from jax.sharding import PartitionSpec as P
from jax.experimental import pallas as pl

D = 2048
CHUNKS = 2


def from_partner(value, axis, distance):
    mask = 2**distance
    pairs = [(source, source ^ mask) for source in range(lax.axis_size(axis))]
    return lax.ppermute(value, axis, pairs)


def ffn_kernel(normed_ref, cot_ref, wg_ref, wu_ref, wd_ref, out_ref):
    cblock = wg_ref.shape[1]
    contract_last = (((1,), (1,)), ((), ()))
    for group in range(wg_ref.shape[0]):
        cols = slice(group * cblock, (group + 1) * cblock)
        normed = normed_ref[:, cols]
        w_gate = wg_ref[group]
        w_up = wu_ref[group]
        gate_pre = jnp.dot(normed, w_gate, preferred_element_type=jnp.float32)
        up_val = jnp.dot(normed, w_up, preferred_element_type=jnp.float32)
        d_hidden = lax.dot_general(
            cot_ref[:, cols], wd_ref[group], contract_last, preferred_element_type=jnp.float32
        )
        sig = 1.0 / (1.0 + jnp.exp(-gate_pre))
        d_up = (d_hidden * gate_pre * sig).astype(jnp.bfloat16)
        d_gate = (d_hidden * up_val * sig * (1.0 + gate_pre * (1.0 - sig))).astype(jnp.bfloat16)
        out_ref[:, cols] = lax.dot_general(
            d_gate, w_gate, contract_last, preferred_element_type=jnp.float32
        ) + lax.dot_general(d_up, w_up, contract_last, preferred_element_type=jnp.float32)


def ffn_grad(normed, cotangent, w_gate, w_up, w_down, per_step=4):
    tok, width = normed.shape
    groups_here, cblock, hidden = w_gate.shape
    if groups_here % per_step:
        per_step = 1
    act = pl.BlockSpec((tok, cblock * per_step), lambda g: (0, g))
    return pl.pallas_call(
        ffn_kernel,
        grid=(groups_here // per_step,),
        in_specs=[
            act,
            act,
            pl.BlockSpec((per_step, cblock, hidden), lambda g: (g, 0, 0)),
            pl.BlockSpec((per_step, cblock, hidden), lambda g: (g, 0, 0)),
            pl.BlockSpec((per_step, hidden, cblock), lambda g: (g, 0, 0)),
        ],
        out_specs=act,
        out_shape=jax.ShapeDtypeStruct((tok, width), jnp.float32),
        cost_estimate=pl.CostEstimate(
            flops=10 * tok * cblock * hidden * groups_here,
            transcendentals=tok * hidden * groups_here,
            bytes_accessed=3 * groups_here * cblock * hidden * 2 + tok * width * 8,
        ),
    )(normed, cotangent, w_gate, w_up, w_down)


def hid_sum_sync(value):
    size = lax.axis_size("hid")
    parts = lax.all_to_all(jnp.stack([value] * size), "hid", 0, 0)
    total = parts[0]
    for index in range(1, size):
        total = total + parts[index]
    return total


def hid_sum(value):
    size = lax.axis_size("hid")
    total = value
    for shift in range(1, size):
        pairs = [(source, (source + shift) % size) for source in range(size)]
        total = total + lax.ppermute(value, "hid", pairs)
    return total


def tie(value, after):
    if after is None:
        return value
    return lax.optimization_barrier((value, after))[0]


def body(tokens, cotangent, blocks, coef_self, coef_cross, norm_gain, w_gate, w_up, w_down):
    tok, width = tokens.shape
    sections = lax.axis_size("seq").bit_length() - 1
    nblk = blocks.shape[0]
    blen = blocks.shape[1]
    tok_blocks = tokens.reshape(nblk, blen, width)
    chunks = CHUNKS if tok % CHUNKS == 0 else 1
    rows = tok // chunks
    spans = [slice(chunk * rows, (chunk + 1) * rows) for chunk in range(chunks)]
    states = [[None] * sections for _ in spans]
    mates = [[None] * sections for _ in spans]
    if nblk == 1:
        pieces = [
            jnp.einsum(
                "kij,kjd->kid", blocks[:, rs], tok_blocks, preferred_element_type=jnp.float32
            ).astype(jnp.bfloat16).reshape(rows, width)
            for rs in spans
        ]
    else:
        local = jnp.einsum(
            "kij,kjd->kid", blocks, tok_blocks, preferred_element_type=jnp.float32
        ).astype(jnp.bfloat16).reshape(tok, width)
        pieces = [local[rs] for rs in spans]
    for section in range(sections):
        for chunk, rs in enumerate(spans):
            value = pieces[chunk]
            mate = from_partner(value, "seq", section)
            states[chunk][section] = value
            mates[chunk][section] = mate
            pieces[chunk] = (
                coef_self[section, rs][:, None] * value.astype(jnp.float32)
                + coef_cross[section, rs][:, None] * mate.astype(jnp.float32)
            ).astype(jnp.bfloat16)
    top = sections - 1
    backs = []
    sents = []
    directs = []
    previous = None
    for chunk, rs in enumerate(spans):
        mixed = tie(pieces[chunk], previous)
        cot = cotangent[rs]
        tok_f = tokens[rs].astype(jnp.float32)
        mixed_f = mixed.astype(jnp.float32)
        resid = tok_f + tok_f * mixed_f
        reduce_hid = hid_sum if chunk == 0 else hid_sum_sync
        square = hid_sum(jnp.sum(resid * resid, axis=-1))
        inv = lax.rsqrt(square / D + 1e-06)
        normed = (resid * inv[:, None] * norm_gain).astype(jnp.bfloat16)
        d_normed = ffn_grad(normed, cot, w_gate, w_up, w_down)
        scaled = norm_gain * d_normed
        inner = reduce_hid(jnp.sum(resid * scaled, axis=-1))
        d_resid = (
            cot.astype(jnp.float32)
            + inv[:, None] * scaled
            - resid * (inv**3 * inner / D)[:, None]
        )
        d_mixed = (d_resid * tok_f).astype(jnp.bfloat16)
        sent = (coef_cross[top, rs][:, None] * d_mixed.astype(jnp.float32)).astype(jnp.bfloat16)
        previous = sent
        backs.append(d_mixed)
        sents.append(from_partner(sent, "seq", top))
        directs.append(d_resid * (1.0 + mixed_f))
    grads_self = [[None] * sections for _ in spans]
    grads_cross = [[None] * sections for _ in spans]
    for section in range(sections - 1, -1, -1):
        for chunk, rs in enumerate(spans):
            back_f = backs[chunk].astype(jnp.float32)
            grads_self[chunk][section] = jnp.sum(
                back_f * states[chunk][section].astype(jnp.float32), axis=-1
            )
            grads_cross[chunk][section] = jnp.sum(
                back_f * mates[chunk][section].astype(jnp.float32), axis=-1
            )
            if section == top:
                received = sents[chunk]
            else:
                sent = (coef_cross[section, rs][:, None] * back_f).astype(jnp.bfloat16)
                received = from_partner(sent, "seq", section)
            backs[chunk] = (
                coef_self[section, rs][:, None] * back_f + received.astype(jnp.float32)
            ).astype(jnp.bfloat16)
    back = jnp.concatenate(backs, axis=0)
    part_self = jnp.concatenate([jnp.stack(g) for g in grads_self], axis=1)
    part_cross = jnp.concatenate([jnp.stack(g) for g in grads_cross], axis=1)
    back_blocks = back.reshape(nblk, blen, width)
    part_blocks = jnp.einsum(
        "kid,kjd->kij", back_blocks, tok_blocks, preferred_element_type=jnp.float32
    )
    from_blocks = jnp.einsum(
        "kij,kid->kjd", blocks, back_blocks, preferred_element_type=jnp.float32
    ).reshape(tok, width)
    grad_self, grad_cross, grad_blocks = jax.tree.map(hid_sum, (part_self, part_cross, part_blocks))
    grad_x = (jnp.concatenate(directs, axis=0) + from_blocks).astype(jnp.bfloat16)
    return (grad_x, grad_self, grad_cross, grad_blocks)


def solution(mesh):
    return jax.shard_map(
        body,
        mesh=mesh,
        in_specs=(
            P(("groups", "seq"), "hid"),
            P(("groups", "seq"), "hid"),
            P("seq", None, None),
            P(None, "seq"),
            P(None, "seq"),
            P("hid"),
            P("hid", None, None),
            P("hid", None, None),
            P("hid", None, None),
        ),
        out_specs=(
            P(("groups", "seq"), "hid"),
            P(None, ("groups", "seq")),
            P(None, ("groups", "seq")),
            P(("groups", "seq"), None, None),
        ),
        check_vma=False,
    )
```

```python
import jax
import jax.numpy as jnp
from jax import lax
from jax.sharding import PartitionSpec as P
from jax.experimental import pallas as pl

D = 2048
CHUNKS = 2
LANES = 128


def from_partner(value, axis, distance):
    mask = 2**distance
    pairs = [(source, source ^ mask) for source in range(lax.axis_size(axis))]
    return lax.ppermute(value, axis, pairs)


def ffn_kernel(normed_ref, cot_ref, wg_ref, wu_ref, wd_ref, out_ref):
    cblock = wg_ref.shape[1]
    contract_last = (((1,), (1,)), ((), ()))
    for group in range(wg_ref.shape[0]):
        cols = slice(group * cblock, (group + 1) * cblock)
        normed = normed_ref[:, cols]
        w_gate = wg_ref[group]
        w_up = wu_ref[group]
        gate_pre = jnp.dot(normed, w_gate, preferred_element_type=jnp.float32)
        up_val = jnp.dot(normed, w_up, preferred_element_type=jnp.float32)
        d_hidden = lax.dot_general(
            cot_ref[:, cols], wd_ref[group], contract_last, preferred_element_type=jnp.float32
        )
        sig = 1.0 / (1.0 + jnp.exp(-gate_pre))
        d_up = (d_hidden * gate_pre * sig).astype(jnp.bfloat16)
        d_gate = (d_hidden * up_val * sig * (1.0 + gate_pre * (1.0 - sig))).astype(jnp.bfloat16)
        out_ref[:, cols] = lax.dot_general(
            d_gate, w_gate, contract_last, preferred_element_type=jnp.float32
        ) + lax.dot_general(d_up, w_up, contract_last, preferred_element_type=jnp.float32)


def ffn_grad(normed, cotangent, w_gate, w_up, w_down, per_step=4):
    tok, width = normed.shape
    groups_here, cblock, hidden = w_gate.shape
    if groups_here % per_step:
        per_step = 1
    act = pl.BlockSpec((tok, cblock * per_step), lambda g: (0, g))
    return pl.pallas_call(
        ffn_kernel,
        grid=(groups_here // per_step,),
        in_specs=[
            act,
            act,
            pl.BlockSpec((per_step, cblock, hidden), lambda g: (g, 0, 0)),
            pl.BlockSpec((per_step, cblock, hidden), lambda g: (g, 0, 0)),
            pl.BlockSpec((per_step, hidden, cblock), lambda g: (g, 0, 0)),
        ],
        out_specs=act,
        out_shape=jax.ShapeDtypeStruct((tok, width), jnp.float32),
        cost_estimate=pl.CostEstimate(
            flops=10 * tok * cblock * hidden * groups_here,
            transcendentals=tok * hidden * groups_here,
            bytes_accessed=3 * groups_here * cblock * hidden * 2 + tok * width * 8,
        ),
    )(normed, cotangent, w_gate, w_up, w_down)


def hid_sum(value):
    size = lax.axis_size("hid")
    total = value
    for shift in range(1, size):
        pairs = [(source, (source + shift) % size) for source in range(size)]
        total = total + lax.ppermute(value, "hid", pairs)
    return total


def tie(value, after):
    if after is None:
        return value
    return lax.optimization_barrier((value, after))[0]


def body(tokens, cotangent, blocks, coef_self, coef_cross, norm_gain, w_gate, w_up, w_down):
    tok, width = tokens.shape
    sections = lax.axis_size("seq").bit_length() - 1
    nblk = blocks.shape[0]
    blen = blocks.shape[1]
    tok_blocks = tokens.reshape(nblk, blen, width)
    chunks = CHUNKS if tok % CHUNKS == 0 else 1
    rows = tok // chunks
    spans = [slice(chunk * rows, (chunk + 1) * rows) for chunk in range(chunks)]
    states = [[None] * sections for _ in spans]
    mates = [[None] * sections for _ in spans]
    if nblk == 1:
        pieces = [
            jnp.einsum(
                "kij,kjd->kid", blocks[:, rs], tok_blocks, preferred_element_type=jnp.float32
            ).astype(jnp.bfloat16).reshape(rows, width)
            for rs in spans
        ]
    else:
        local = jnp.einsum(
            "kij,kjd->kid", blocks, tok_blocks, preferred_element_type=jnp.float32
        ).astype(jnp.bfloat16).reshape(tok, width)
        pieces = [local[rs] for rs in spans]
    for section in range(sections):
        for chunk, rs in enumerate(spans):
            value = pieces[chunk]
            mate = from_partner(value, "seq", section)
            states[chunk][section] = value
            mates[chunk][section] = mate
            pieces[chunk] = (
                coef_self[section, rs][:, None] * value.astype(jnp.float32)
                + coef_cross[section, rs][:, None] * mate.astype(jnp.float32)
            ).astype(jnp.bfloat16)
    top = sections - 1
    backs = []
    sents = []
    directs = []
    previous = None
    for chunk, rs in enumerate(spans):
        mixed = tie(pieces[chunk], previous)
        cot = cotangent[rs]
        tok_f = tokens[rs].astype(jnp.float32)
        mixed_f = mixed.astype(jnp.float32)
        resid = tok_f + tok_f * mixed_f
        reduce_hid = hid_sum if chunk == 0 else (lambda v: lax.psum(v, "hid"))
        square = hid_sum(jnp.sum(resid * resid, axis=-1))
        inv = lax.rsqrt(square / D + 1e-06)
        normed = (resid * inv[:, None] * norm_gain).astype(jnp.bfloat16)
        d_normed = ffn_grad(normed, cot, w_gate, w_up, w_down)
        scaled = norm_gain * d_normed
        lanes = jnp.sum((resid * scaled).reshape(resid.shape[0], -1, LANES), axis=1)
        inner = reduce_hid(jnp.sum(lax.optimization_barrier(lanes), axis=-1))
        d_resid = (
            cot.astype(jnp.float32)
            + inv[:, None] * scaled
            - resid * (inv**3 * inner / D)[:, None]
        )
        d_mixed = (d_resid * tok_f).astype(jnp.bfloat16)
        sent = (coef_cross[top, rs][:, None] * d_mixed.astype(jnp.float32)).astype(jnp.bfloat16)
        previous = sent
        backs.append(d_mixed)
        sents.append(from_partner(sent, "seq", top))
        directs.append(d_resid * (1.0 + mixed_f))
    grads_self = [[None] * sections for _ in spans]
    grads_cross = [[None] * sections for _ in spans]
    for section in range(sections - 1, -1, -1):
        for chunk, rs in enumerate(spans):
            back_f = backs[chunk].astype(jnp.float32)
            grads_self[chunk][section] = jnp.sum(
                back_f * states[chunk][section].astype(jnp.float32), axis=-1
            )
            grads_cross[chunk][section] = jnp.sum(
                back_f * mates[chunk][section].astype(jnp.float32), axis=-1
            )
            if section == top:
                received = sents[chunk]
            else:
                sent = (coef_cross[section, rs][:, None] * back_f).astype(jnp.bfloat16)
                received = from_partner(sent, "seq", section)
            backs[chunk] = (
                coef_self[section, rs][:, None] * back_f + received.astype(jnp.float32)
            ).astype(jnp.bfloat16)
    back = jnp.concatenate(backs, axis=0)
    part_self = jnp.concatenate([jnp.stack(g) for g in grads_self], axis=1)
    part_cross = jnp.concatenate([jnp.stack(g) for g in grads_cross], axis=1)
    back_blocks = back.reshape(nblk, blen, width)
    part_blocks = jnp.einsum(
        "kid,kjd->kij", back_blocks, tok_blocks, preferred_element_type=jnp.float32
    )
    from_blocks = jnp.einsum(
        "kij,kid->kjd", blocks, back_blocks, preferred_element_type=jnp.float32
    ).reshape(tok, width)
    grad_self, grad_cross, grad_blocks = jax.tree.map(hid_sum, (part_self, part_cross, part_blocks))
    grad_x = (jnp.concatenate(directs, axis=0) + from_blocks).astype(jnp.bfloat16)
    return (grad_x, grad_self, grad_cross, grad_blocks)


def solution(mesh):
    return jax.shard_map(
        body,
        mesh=mesh,
        in_specs=(
            P(("groups", "seq"), "hid"),
            P(("groups", "seq"), "hid"),
            P("seq", None, None),
            P(None, "seq"),
            P(None, "seq"),
            P("hid"),
            P("hid", None, None),
            P("hid", None, None),
            P("hid", None, None),
        ),
        out_specs=(
            P(("groups", "seq"), "hid"),
            P(None, ("groups", "seq")),
            P(None, ("groups", "seq")),
            P(("groups", "seq"), None, None),
        ),
        check_vma=False,
    )
```

```python
import jax
import jax.numpy as jnp
from jax import lax
from jax.sharding import PartitionSpec as P
from jax.experimental import pallas as pl

D = 2048
CHUNKS = 2


def from_partner(value, axis, distance):
    mask = 2**distance
    pairs = [(source, source ^ mask) for source in range(lax.axis_size(axis))]
    return lax.ppermute(value, axis, pairs)


def ffn_kernel(normed_ref, cot_ref, tok_ref, mix_ref, gain_ref, wg_ref, wu_ref, wd_ref,
               out_ref, acc_ref):
    cblock = wg_ref.shape[1]
    contract_last = (((1,), (1,)), ((), ()))
    acc = jnp.zeros(acc_ref.shape, jnp.float32)
    for group in range(wg_ref.shape[0]):
        cols = slice(group * cblock, (group + 1) * cblock)
        normed = normed_ref[:, cols]
        w_gate = wg_ref[group]
        w_up = wu_ref[group]
        gate_pre = jnp.dot(normed, w_gate, preferred_element_type=jnp.float32)
        up_val = jnp.dot(normed, w_up, preferred_element_type=jnp.float32)
        d_hidden = lax.dot_general(
            cot_ref[:, cols], wd_ref[group], contract_last, preferred_element_type=jnp.float32
        )
        sig = 1.0 / (1.0 + jnp.exp(-gate_pre))
        d_up = (d_hidden * gate_pre * sig).astype(jnp.bfloat16)
        d_gate = (d_hidden * up_val * sig * (1.0 + gate_pre * (1.0 - sig))).astype(jnp.bfloat16)
        d_normed = lax.dot_general(
            d_gate, w_gate, contract_last, preferred_element_type=jnp.float32
        ) + lax.dot_general(d_up, w_up, contract_last, preferred_element_type=jnp.float32)
        out_ref[:, cols] = d_normed
        tok = tok_ref[:, cols].astype(jnp.float32)
        resid = tok + tok * mix_ref[:, cols].astype(jnp.float32)
        acc = acc + resid * (gain_ref[:, cols] * d_normed)

    @pl.when(pl.program_id(0) == 0)
    def _():
        acc_ref[...] = acc

    @pl.when(pl.program_id(0) > 0)
    def _():
        acc_ref[...] += acc


def ffn_grad(normed, cotangent, tokens, mixed, norm_gain, w_gate, w_up, w_down, per_step=4):
    tok, width = normed.shape
    groups_here, cblock, hidden = w_gate.shape
    if groups_here % per_step:
        per_step = 1
    act = pl.BlockSpec((tok, cblock * per_step), lambda g: (0, g))
    return pl.pallas_call(
        ffn_kernel,
        grid=(groups_here // per_step,),
        in_specs=[
            act,
            act,
            act,
            act,
            pl.BlockSpec((1, cblock * per_step), lambda g: (0, g)),
            pl.BlockSpec((per_step, cblock, hidden), lambda g: (g, 0, 0)),
            pl.BlockSpec((per_step, cblock, hidden), lambda g: (g, 0, 0)),
            pl.BlockSpec((per_step, hidden, cblock), lambda g: (g, 0, 0)),
        ],
        out_specs=[act, pl.BlockSpec((tok, cblock), lambda g: (0, 0))],
        out_shape=[
            jax.ShapeDtypeStruct((tok, width), jnp.float32),
            jax.ShapeDtypeStruct((tok, cblock), jnp.float32),
        ],
        cost_estimate=pl.CostEstimate(
            flops=10 * tok * cblock * hidden * groups_here,
            transcendentals=tok * hidden * groups_here,
            bytes_accessed=3 * groups_here * cblock * hidden * 2 + tok * width * 12,
        ),
    )(normed, cotangent, tokens, mixed, norm_gain[None, :], w_gate, w_up, w_down)


def hid_sum(value):
    size = lax.axis_size("hid")
    total = value
    for shift in range(1, size):
        pairs = [(source, (source + shift) % size) for source in range(size)]
        total = total + lax.ppermute(value, "hid", pairs)
    return total


def tie(value, after):
    if after is None:
        return value
    return lax.optimization_barrier((value, after))[0]


def body(tokens, cotangent, blocks, coef_self, coef_cross, norm_gain, w_gate, w_up, w_down):
    tok, width = tokens.shape
    sections = lax.axis_size("seq").bit_length() - 1
    nblk = blocks.shape[0]
    blen = blocks.shape[1]
    tok_blocks = tokens.reshape(nblk, blen, width)
    chunks = CHUNKS if tok % CHUNKS == 0 else 1
    rows = tok // chunks
    spans = [slice(chunk * rows, (chunk + 1) * rows) for chunk in range(chunks)]
    states = [[None] * sections for _ in spans]
    mates = [[None] * sections for _ in spans]
    if nblk == 1:
        pieces = [
            jnp.einsum(
                "kij,kjd->kid", blocks[:, rs], tok_blocks, preferred_element_type=jnp.float32
            ).astype(jnp.bfloat16).reshape(rows, width)
            for rs in spans
        ]
    else:
        local = jnp.einsum(
            "kij,kjd->kid", blocks, tok_blocks, preferred_element_type=jnp.float32
        ).astype(jnp.bfloat16).reshape(tok, width)
        pieces = [local[rs] for rs in spans]
    for section in range(sections):
        for chunk, rs in enumerate(spans):
            value = pieces[chunk]
            mate = from_partner(value, "seq", section)
            states[chunk][section] = value
            mates[chunk][section] = mate
            pieces[chunk] = (
                coef_self[section, rs][:, None] * value.astype(jnp.float32)
                + coef_cross[section, rs][:, None] * mate.astype(jnp.float32)
            ).astype(jnp.bfloat16)
    top = sections - 1
    backs = []
    sents = []
    directs = []
    previous = None
    for chunk, rs in enumerate(spans):
        mixed = tie(pieces[chunk], previous)
        cot = cotangent[rs]
        tok_f = tokens[rs].astype(jnp.float32)
        mixed_f = mixed.astype(jnp.float32)
        resid = tok_f + tok_f * mixed_f
        reduce_hid = hid_sum if chunk == 0 else (lambda v: lax.psum(v, "hid"))
        square = hid_sum(jnp.sum(resid * resid, axis=-1))
        inv = lax.rsqrt(square / D + 1e-06)
        normed = (resid * inv[:, None] * norm_gain).astype(jnp.bfloat16)
        d_normed, lanes = ffn_grad(
            normed, cot, tokens[rs], mixed, norm_gain, w_gate, w_up, w_down
        )
        scaled = norm_gain * d_normed
        inner = reduce_hid(jnp.sum(lanes, axis=-1))
        d_resid = (
            cot.astype(jnp.float32)
            + inv[:, None] * scaled
            - resid * (inv**3 * inner / D)[:, None]
        )
        d_mixed = (d_resid * tok_f).astype(jnp.bfloat16)
        sent = (coef_cross[top, rs][:, None] * d_mixed.astype(jnp.float32)).astype(jnp.bfloat16)
        previous = sent
        backs.append(d_mixed)
        sents.append(from_partner(sent, "seq", top))
        directs.append(d_resid * (1.0 + mixed_f))
    grads_self = [[None] * sections for _ in spans]
    grads_cross = [[None] * sections for _ in spans]
    for section in range(sections - 1, -1, -1):
        for chunk, rs in enumerate(spans):
            back_f = backs[chunk].astype(jnp.float32)
            grads_self[chunk][section] = jnp.sum(
                back_f * states[chunk][section].astype(jnp.float32), axis=-1
            )
            grads_cross[chunk][section] = jnp.sum(
                back_f * mates[chunk][section].astype(jnp.float32), axis=-1
            )
            if section == top:
                received = sents[chunk]
            else:
                sent = (coef_cross[section, rs][:, None] * back_f).astype(jnp.bfloat16)
                received = from_partner(sent, "seq", section)
            backs[chunk] = (
                coef_self[section, rs][:, None] * back_f + received.astype(jnp.float32)
            ).astype(jnp.bfloat16)
    back = jnp.concatenate(backs, axis=0)
    part_self = jnp.concatenate([jnp.stack(g) for g in grads_self], axis=1)
    part_cross = jnp.concatenate([jnp.stack(g) for g in grads_cross], axis=1)
    back_blocks = back.reshape(nblk, blen, width)
    part_blocks = jnp.einsum(
        "kid,kjd->kij", back_blocks, tok_blocks, preferred_element_type=jnp.float32
    )
    from_blocks = jnp.einsum(
        "kij,kid->kjd", blocks, back_blocks, preferred_element_type=jnp.float32
    ).reshape(tok, width)
    grad_self, grad_cross, grad_blocks = jax.tree.map(hid_sum, (part_self, part_cross, part_blocks))
    grad_x = (jnp.concatenate(directs, axis=0) + from_blocks).astype(jnp.bfloat16)
    return (grad_x, grad_self, grad_cross, grad_blocks)


def solution(mesh):
    return jax.shard_map(
        body,
        mesh=mesh,
        in_specs=(
            P(("groups", "seq"), "hid"),
            P(("groups", "seq"), "hid"),
            P("seq", None, None),
            P(None, "seq"),
            P(None, "seq"),
            P("hid"),
            P("hid", None, None),
            P("hid", None, None),
            P("hid", None, None),
        ),
        out_specs=(
            P(("groups", "seq"), "hid"),
            P(None, ("groups", "seq")),
            P(None, ("groups", "seq")),
            P(("groups", "seq"), None, None),
        ),
        check_vma=False,
    )
```

```python
import jax
import jax.numpy as jnp
from jax import lax
from jax.sharding import PartitionSpec as P
from jax.experimental import pallas as pl

D = 2048
CHUNKS = 2


def from_partner(value, axis, distance):
    mask = 2**distance
    pairs = [(source, source ^ mask) for source in range(lax.axis_size(axis))]
    return lax.ppermute(value, axis, pairs)


def ffn_kernel(normed_ref, cot_ref, wg_ref, wu_ref, wd_ref, out_ref):
    cblock = wg_ref.shape[1]
    contract_last = (((1,), (1,)), ((), ()))
    for group in range(wg_ref.shape[0]):
        cols = slice(group * cblock, (group + 1) * cblock)
        normed = normed_ref[:, cols]
        w_gate = wg_ref[group]
        w_up = wu_ref[group]
        gate_pre = jnp.dot(normed, w_gate, preferred_element_type=jnp.float32)
        up_val = jnp.dot(normed, w_up, preferred_element_type=jnp.float32)
        d_hidden = lax.dot_general(
            cot_ref[:, cols], wd_ref[group], contract_last, preferred_element_type=jnp.float32
        )
        sig = 1.0 / (1.0 + jnp.exp(-gate_pre))
        d_up = (d_hidden * gate_pre * sig).astype(jnp.bfloat16)
        d_gate = (d_hidden * up_val * sig * (1.0 + gate_pre * (1.0 - sig))).astype(jnp.bfloat16)
        out_ref[:, cols] = (
            lax.dot_general(d_gate, w_gate, contract_last, preferred_element_type=jnp.float32)
            + lax.dot_general(d_up, w_up, contract_last, preferred_element_type=jnp.float32)
        ).astype(out_ref.dtype)


def ffn_grad(normed, cotangent, w_gate, w_up, w_down, per_step=4):
    tok, width = normed.shape
    groups_here, cblock, hidden = w_gate.shape
    if groups_here % per_step:
        per_step = 1
    act = pl.BlockSpec((tok, cblock * per_step), lambda g: (0, g))
    return pl.pallas_call(
        ffn_kernel,
        grid=(groups_here // per_step,),
        in_specs=[
            act,
            act,
            pl.BlockSpec((per_step, cblock, hidden), lambda g: (g, 0, 0)),
            pl.BlockSpec((per_step, cblock, hidden), lambda g: (g, 0, 0)),
            pl.BlockSpec((per_step, hidden, cblock), lambda g: (g, 0, 0)),
        ],
        out_specs=act,
        out_shape=jax.ShapeDtypeStruct((tok, width), jnp.bfloat16),
        cost_estimate=pl.CostEstimate(
            flops=10 * tok * cblock * hidden * groups_here,
            transcendentals=tok * hidden * groups_here,
            bytes_accessed=3 * groups_here * cblock * hidden * 2 + tok * width * 8,
        ),
    )(normed, cotangent, w_gate, w_up, w_down)


def hid_sum(value):
    size = lax.axis_size("hid")
    total = value
    for shift in range(1, size):
        pairs = [(source, (source + shift) % size) for source in range(size)]
        total = total + lax.ppermute(value, "hid", pairs)
    return total


def tie(value, after):
    if after is None:
        return value
    return lax.optimization_barrier((value, after))[0]


def body(tokens, cotangent, blocks, coef_self, coef_cross, norm_gain, w_gate, w_up, w_down):
    tok, width = tokens.shape
    sections = lax.axis_size("seq").bit_length() - 1
    nblk = blocks.shape[0]
    blen = blocks.shape[1]
    tok_blocks = tokens.reshape(nblk, blen, width)
    chunks = CHUNKS if tok % CHUNKS == 0 else 1
    rows = tok // chunks
    spans = [slice(chunk * rows, (chunk + 1) * rows) for chunk in range(chunks)]
    states = [[None] * sections for _ in spans]
    mates = [[None] * sections for _ in spans]
    if nblk == 1:
        pieces = [
            jnp.einsum(
                "kij,kjd->kid", blocks[:, rs], tok_blocks, preferred_element_type=jnp.float32
            ).astype(jnp.bfloat16).reshape(rows, width)
            for rs in spans
        ]
    else:
        local = jnp.einsum(
            "kij,kjd->kid", blocks, tok_blocks, preferred_element_type=jnp.float32
        ).astype(jnp.bfloat16).reshape(tok, width)
        pieces = [local[rs] for rs in spans]
    for section in range(sections):
        for chunk, rs in enumerate(spans):
            value = pieces[chunk]
            mate = from_partner(value, "seq", section)
            states[chunk][section] = value
            mates[chunk][section] = mate
            pieces[chunk] = (
                coef_self[section, rs][:, None] * value.astype(jnp.float32)
                + coef_cross[section, rs][:, None] * mate.astype(jnp.float32)
            ).astype(jnp.bfloat16)
    top = sections - 1
    backs = []
    sents = []
    directs = []
    previous = None
    for chunk, rs in enumerate(spans):
        mixed = tie(pieces[chunk], previous)
        cot = cotangent[rs]
        tok_f = tokens[rs].astype(jnp.float32)
        mixed_f = mixed.astype(jnp.float32)
        resid = tok_f + tok_f * mixed_f
        reduce_hid = hid_sum if chunk == 0 else (lambda v: lax.psum(v, "hid"))
        square = hid_sum(jnp.sum(resid * resid, axis=-1))
        inv = lax.rsqrt(square / D + 1e-06)
        normed = (resid * inv[:, None] * norm_gain).astype(jnp.bfloat16)
        d_normed = ffn_grad(normed, cot, w_gate, w_up, w_down)
        scaled = norm_gain * d_normed
        inner = reduce_hid(jnp.sum(resid * scaled, axis=-1))
        d_resid = (
            cot.astype(jnp.float32)
            + inv[:, None] * scaled
            - resid * (inv**3 * inner / D)[:, None]
        )
        d_mixed = (d_resid * tok_f).astype(jnp.bfloat16)
        sent = (coef_cross[top, rs][:, None] * d_mixed.astype(jnp.float32)).astype(jnp.bfloat16)
        previous = sent
        backs.append(d_mixed)
        sents.append(from_partner(sent, "seq", top))
        directs.append(d_resid * (1.0 + mixed_f))
    grads_self = [[None] * sections for _ in spans]
    grads_cross = [[None] * sections for _ in spans]
    for section in range(sections - 1, -1, -1):
        for chunk, rs in enumerate(spans):
            back_f = backs[chunk].astype(jnp.float32)
            grads_self[chunk][section] = jnp.sum(
                back_f * states[chunk][section].astype(jnp.float32), axis=-1
            )
            grads_cross[chunk][section] = jnp.sum(
                back_f * mates[chunk][section].astype(jnp.float32), axis=-1
            )
            if section == top:
                received = sents[chunk]
            else:
                sent = (coef_cross[section, rs][:, None] * back_f).astype(jnp.bfloat16)
                received = from_partner(sent, "seq", section)
            backs[chunk] = (
                coef_self[section, rs][:, None] * back_f + received.astype(jnp.float32)
            ).astype(jnp.bfloat16)
    back = jnp.concatenate(backs, axis=0)
    part_self = jnp.concatenate([jnp.stack(g) for g in grads_self], axis=1)
    part_cross = jnp.concatenate([jnp.stack(g) for g in grads_cross], axis=1)
    back_blocks = back.reshape(nblk, blen, width)
    part_blocks = jnp.einsum(
        "kid,kjd->kij", back_blocks, tok_blocks, preferred_element_type=jnp.float32
    )
    from_blocks = jnp.einsum(
        "kij,kid->kjd", blocks, back_blocks, preferred_element_type=jnp.float32
    ).reshape(tok, width)
    grad_self, grad_cross, grad_blocks = jax.tree.map(hid_sum, (part_self, part_cross, part_blocks))
    grad_x = (jnp.concatenate(directs, axis=0) + from_blocks).astype(jnp.bfloat16)
    return (grad_x, grad_self, grad_cross, grad_blocks)


def solution(mesh):
    return jax.shard_map(
        body,
        mesh=mesh,
        in_specs=(
            P(("groups", "seq"), "hid"),
            P(("groups", "seq"), "hid"),
            P("seq", None, None),
            P(None, "seq"),
            P(None, "seq"),
            P("hid"),
            P("hid", None, None),
            P("hid", None, None),
            P("hid", None, None),
        ),
        out_specs=(
            P(("groups", "seq"), "hid"),
            P(None, ("groups", "seq")),
            P(None, ("groups", "seq")),
            P(("groups", "seq"), None, None),
        ),
        check_vma=False,
    )
```

```python
import jax
import jax.numpy as jnp
from jax import lax
from jax.sharding import PartitionSpec as P
from jax.experimental import pallas as pl

D = 2048
CHUNKS = 2


def from_partner(value, axis, distance):
    mask = 2**distance
    pairs = [(source, source ^ mask) for source in range(lax.axis_size(axis))]
    return lax.ppermute(value, axis, pairs)


def ffn_kernel(normed_ref, cot_ref, wg_ref, wu_ref, wd_ref, out_ref):
    cblock = wg_ref.shape[1]
    contract_last = (((1,), (1,)), ((), ()))
    for group in range(wg_ref.shape[0]):
        cols = slice(group * cblock, (group + 1) * cblock)
        normed = normed_ref[:, cols]
        w_gate = wg_ref[group]
        w_up = wu_ref[group]
        gate_pre = jnp.dot(normed, w_gate, preferred_element_type=jnp.float32)
        up_val = jnp.dot(normed, w_up, preferred_element_type=jnp.float32)
        d_hidden = lax.dot_general(
            cot_ref[:, cols], wd_ref[group], contract_last, preferred_element_type=jnp.float32
        )
        sig = 1.0 / (1.0 + jnp.exp(-gate_pre))
        d_up = (d_hidden * gate_pre * sig).astype(jnp.bfloat16)
        d_gate = (d_hidden * up_val * sig * (1.0 + gate_pre * (1.0 - sig))).astype(jnp.bfloat16)
        out_ref[:, cols] = lax.dot_general(
            d_gate, w_gate, contract_last, preferred_element_type=jnp.float32
        ) + lax.dot_general(d_up, w_up, contract_last, preferred_element_type=jnp.float32)


def ffn_grad(normed, cotangent, w_gate, w_up, w_down, per_step=4):
    tok, width = normed.shape
    groups_here, cblock, hidden = w_gate.shape
    if groups_here % per_step:
        per_step = 1
    act = pl.BlockSpec((tok, cblock * per_step), lambda g: (0, g))
    return pl.pallas_call(
        ffn_kernel,
        grid=(groups_here // per_step,),
        in_specs=[
            act,
            act,
            pl.BlockSpec((per_step, cblock, hidden), lambda g: (g, 0, 0)),
            pl.BlockSpec((per_step, cblock, hidden), lambda g: (g, 0, 0)),
            pl.BlockSpec((per_step, hidden, cblock), lambda g: (g, 0, 0)),
        ],
        out_specs=act,
        out_shape=jax.ShapeDtypeStruct((tok, width), jnp.float32),
        cost_estimate=pl.CostEstimate(
            flops=10 * tok * cblock * hidden * groups_here,
            transcendentals=tok * hidden * groups_here,
            bytes_accessed=3 * groups_here * cblock * hidden * 2 + tok * width * 8,
        ),
    )(normed, cotangent, w_gate, w_up, w_down)


def hid_sum(value):
    size = lax.axis_size("hid")
    total = value
    for shift in range(1, size):
        pairs = [(source, (source + shift) % size) for source in range(size)]
        total = total + lax.ppermute(value, "hid", pairs)
    return total


def tie(value, after):
    if after is None:
        return value
    return lax.optimization_barrier((value, after))[0]


def body(tokens, cotangent, blocks, coef_self, coef_cross, norm_gain, w_gate, w_up, w_down):
    tok, width = tokens.shape
    sections = lax.axis_size("seq").bit_length() - 1
    nblk = blocks.shape[0]
    blen = blocks.shape[1]
    tok_blocks = tokens.reshape(nblk, blen, width)
    chunks = CHUNKS if tok % CHUNKS == 0 else 1
    rows = tok // chunks
    spans = [slice(chunk * rows, (chunk + 1) * rows) for chunk in range(chunks)]
    states = [[None] * sections for _ in spans]
    mates = [[None] * sections for _ in spans]
    if nblk == 1:
        pieces = [
            jnp.einsum(
                "kij,kjd->kid", blocks[:, rs], tok_blocks, preferred_element_type=jnp.float32
            ).astype(jnp.bfloat16).reshape(rows, width)
            for rs in spans
        ]
    else:
        local = jnp.einsum(
            "kij,kjd->kid", blocks, tok_blocks, preferred_element_type=jnp.float32
        ).astype(jnp.bfloat16).reshape(tok, width)
        pieces = [local[rs] for rs in spans]
    for section in range(sections):
        for chunk, rs in enumerate(spans):
            value = pieces[chunk]
            mate = from_partner(value, "seq", section)
            states[chunk][section] = value
            mates[chunk][section] = mate
            pieces[chunk] = (
                coef_self[section, rs][:, None] * value.astype(jnp.float32)
                + coef_cross[section, rs][:, None] * mate.astype(jnp.float32)
            ).astype(jnp.bfloat16)
    top = sections - 1
    backs = []
    sents = []
    directs = []
    previous = None
    held = None
    for chunk, rs in enumerate(spans):
        mixed = tie(pieces[chunk], previous)
        cot = cotangent[rs]
        tok_f = tokens[rs].astype(jnp.float32)
        mixed_f = mixed.astype(jnp.float32)
        resid = tok_f + tok_f * mixed_f
        square = hid_sum(jnp.sum(resid * resid, axis=-1))
        inv = lax.rsqrt(square / D + 1e-06)
        normed = (resid * inv[:, None] * norm_gain).astype(jnp.bfloat16)
        d_normed = ffn_grad(normed, cot, w_gate, w_up, w_down)
        scaled = norm_gain * d_normed
        partial = jnp.sum(resid * scaled, axis=-1)
        if held is not None:
            partial = tie(partial, held[0])
        inner = hid_sum(partial)
        if held is not None:
            rest = from_partner(tie(held[1], inner), "seq", top)
            sents[-1] = jnp.concatenate([held[0], rest], axis=1)
            held = None
        d_resid = (
            cot.astype(jnp.float32)
            + inv[:, None] * scaled
            - resid * (inv**3 * inner / D)[:, None]
        )
        d_mixed = (d_resid * tok_f).astype(jnp.bfloat16)
        sent = (coef_cross[top, rs][:, None] * d_mixed.astype(jnp.float32)).astype(jnp.bfloat16)
        previous = sent
        backs.append(d_mixed)
        half = width // 2
        if chunk + 1 < len(spans) and half % 128 == 0:
            first_half = from_partner(sent[:, :half], "seq", top)
            held = (first_half, sent[:, half:])
            sents.append(None)
        else:
            sents.append(from_partner(sent, "seq", top))
        directs.append(d_resid * (1.0 + mixed_f))
    grads_self = [[None] * sections for _ in spans]
    grads_cross = [[None] * sections for _ in spans]
    for section in range(sections - 1, -1, -1):
        for chunk, rs in enumerate(spans):
            back_f = backs[chunk].astype(jnp.float32)
            grads_self[chunk][section] = jnp.sum(
                back_f * states[chunk][section].astype(jnp.float32), axis=-1
            )
            grads_cross[chunk][section] = jnp.sum(
                back_f * mates[chunk][section].astype(jnp.float32), axis=-1
            )
            if section == top:
                received = sents[chunk]
            else:
                sent = (coef_cross[section, rs][:, None] * back_f).astype(jnp.bfloat16)
                received = from_partner(sent, "seq", section)
            backs[chunk] = (
                coef_self[section, rs][:, None] * back_f + received.astype(jnp.float32)
            ).astype(jnp.bfloat16)
    back = jnp.concatenate(backs, axis=0)
    part_self = jnp.concatenate([jnp.stack(g) for g in grads_self], axis=1)
    part_cross = jnp.concatenate([jnp.stack(g) for g in grads_cross], axis=1)
    back_blocks = back.reshape(nblk, blen, width)
    part_blocks = jnp.einsum(
        "kid,kjd->kij", back_blocks, tok_blocks, preferred_element_type=jnp.float32
    )
    from_blocks = jnp.einsum(
        "kij,kid->kjd", blocks, back_blocks, preferred_element_type=jnp.float32
    ).reshape(tok, width)
    grad_self, grad_cross, grad_blocks = jax.tree.map(hid_sum, (part_self, part_cross, part_blocks))
    grad_x = (jnp.concatenate(directs, axis=0) + from_blocks).astype(jnp.bfloat16)
    return (grad_x, grad_self, grad_cross, grad_blocks)


def solution(mesh):
    return jax.shard_map(
        body,
        mesh=mesh,
        in_specs=(
            P(("groups", "seq"), "hid"),
            P(("groups", "seq"), "hid"),
            P("seq", None, None),
            P(None, "seq"),
            P(None, "seq"),
            P("hid"),
            P("hid", None, None),
            P("hid", None, None),
            P("hid", None, None),
        ),
        out_specs=(
            P(("groups", "seq"), "hid"),
            P(None, ("groups", "seq")),
            P(None, ("groups", "seq")),
            P(("groups", "seq"), None, None),
        ),
        check_vma=False,
    )
```
